128 devices in a mesh: ep: 128 (over y, z, x, core).
Axes of the slice: x: 4, y: 4, z: 4, core: 2. Of those that a mesh axis runs over, the one named last changes fastest.
Arguments:
- tokens: bfloat16 [16384, 2048], P('ep'), may hold values from -6 to 6
- cotangent: bfloat16 [16384, 2048], P('ep'), may hold values from -1 to 1
- gates: float32 [16384, 8], P('ep'), may hold values from 0.1 to 1
- experts: int32 [16384, 8], P('ep'), may hold values from 0 to 127, all different within a row; in each aligned block of 128 rows (0 to 127, 128 to 255, ...) at most 12 rows name the same one
- owner: int32 [128], replicated, may hold values from 0 to 127, each once
- swapped: int32 [64], replicated, may hold values 0 or 1
- w_gate: bfloat16 [128, 2048, 768], P('ep'), may hold values from -0.125 to 0.125
- w_up: bfloat16 [128, 2048, 768], P('ep'), may hold values from -0.125 to 0.125
- w_down: bfloat16 [128, 768, 2048], P('ep'), may hold values from -0.21875 to 0.21875
Outputs:
- mixed: bfloat16 [16384, 2048], P('ep')
- in_grad: bfloat16 [16384, 2048], P('ep')
- gate_grad: float32 [16384, 8], P('ep')
The draws below stay inside these ranges and needn't reach their ends.
Inputs may be any that keep to these rules, and one draw needn't show every extreme that they name: Each row names 8 different experts. In the rows of one device no expert is named by more than 12 rows, and in every draw some expert is named by exactly 12 rows of some device. `owner`: names each device index once.
All inputs are finite; a program needn't handle non-finite values.
Results may differ from the reference program's by a relative error of at most 0.0065.
Values may be sent and summed in bfloat16 or wider, within the bound.
No kernel may reach another device: no remote copies, remote signals or barrier semaphores. Data moves between devices by JAX's collectives and lax.ppermute only.
A program may use at most 192 MiB of HBM per device.

```python
import math
import jax
import jax.numpy as jnp
import numpy as np
from jax import lax

D = 2048
FF = 768
TOP = 8
TOK_DEV = 128
EXPERTS = 128
CAP = 12
TOKENS = 16384
PAIRS = 64
N_EP = 128


def plant(drawn, rng, low, high):
    index_at = [jax.random.randint(jax.random.fold_in(rng, axis), (), 0, length) for axis, length in enumerate(drawn.shape)]
    longest = drawn.shape.index(max(drawn.shape))
    next_to = index_at[:longest] + [(index_at[longest] + 1) % drawn.shape[longest]] + index_at[longest + 1:]
    return drawn.at[tuple(index_at)].set(low).at[tuple(next_to)].set(high)


def levels(rng, extent, cuts, least, top_value):
    level = 1.0
    for axis_at, shards_of in cuts:
        heights = jax.random.uniform(jax.random.fold_in(jax.random.fold_in(rng, 6), axis_at), (shards_of,), jnp.float32, least / len(cuts), top_value / len(cuts))
        level = level * jnp.repeat(jnp.exp(heights), extent[axis_at] // shards_of).reshape((-1,) + (1,) * (len(extent) - 1 - axis_at))
    return level


def deal_out(rng, own, number, rows, amount, top, most, lean):
    order = jax.random.permutation(rng, amount)
    crowded, common = portions_of(amount, rows * top, most, lean, True), portions_of(amount, rows * top, most, lean, False)
    places = jnp.arange(amount)

    def named(tallies, rotation):
        used = int((tallies > 0).sum())
        fixed = max(1, used // 4)
        shifted = fixed + (places - fixed + rotation * (used - fixed)) % max(1, amount - fixed)
        return jnp.zeros((amount,), jnp.int32).at[order[jnp.where(places < fixed, places, shifted)]].set(jnp.asarray(tallies, jnp.int32))

    tallies = jnp.where(number % 4 == 0, named(crowded, number // 4), named(common, number - number // 4 - 1))
    mixed = jax.random.permutation(jax.random.fold_in(own, 3), amount)
    source_of, receiver = mixed[0:amount // 2 * 2:2], mixed[1:amount // 2 * 2:2]
    slack = jnp.minimum(tallies[source_of] - 1, most - tallies[receiver]) // 2
    slack = jnp.where((source_of == order[0]) | (receiver == order[0]) | (tallies[receiver] == 0), 0, jnp.maximum(slack, 0))
    shifted = jax.random.randint(jax.random.fold_in(own, 4), (amount // 2,), 0, 1 << 20) % (slack + 1)
    tallies = tallies.at[source_of].add(-shifted).at[receiver].add(shifted)
    labels = jnp.searchsorted(jnp.cumsum(tallies), jnp.arange(rows * top), side="right").astype(jnp.int32)
    grid = labels.reshape(top, rows).T
    grid = grid[jax.random.permutation(jax.random.fold_in(own, 1), rows)]
    rotation = jax.random.randint(jax.random.fold_in(own, 2), (rows, 1), 0, top)
    return jnp.take_along_axis(grid, (jnp.arange(top)[None, :] + rotation) % top, axis=1)


def portions_of(number_of, total, reach, slope, full):
    portions = [(1 << 20) // math.isqrt(grade ** slope) + 1 for grade in range(1, number_of + 1)]
    largest = reach if full else min(reach, max(-(-total // number_of), total * portions[0] // sum(portions)))
    least = 1 if total - largest >= number_of - 1 else 0
    holding, surplus = [largest] + [least] * (number_of - 1), total - largest - least * (number_of - 1)
    while surplus > 0:
        free = [i for i in range(1, number_of) if holding[i] < largest] or [i for i in range(1, number_of) if holding[i] < reach]
        mass, budget = sum([portions[i] for i in free]), surplus
        for i in free:
            extra = min(reach - holding[i], max(1, budget * portions[i] // mass), surplus)
            holding[i] = holding[i] + extra
            surplus = surplus - extra
    return np.array(holding)


def bell_draw(key, extent, scale, bound, cuts=(), held_as=jnp.bfloat16):
    values = scale * jax.random.normal(key, extent, jnp.float32)
    if cuts:
        values = values * levels(key, extent, cuts, -0.22, 0.18)
    return jnp.clip(values, -bound, bound).astype(held_as)


def setup_inputs(seed: int = 0) -> dict:
    key_list = jax.random.split(jax.random.key(seed), 10)
    tokens = bell_draw(key_list[0], (TOKENS, D), 1.0, 6.0, ((0, 128),))
    cotangent = bell_draw(key_list[1], (TOKENS, D), 0.15, 1.0, ((0, 128),))
    gates = jnp.clip(0.1 + 0.9 * jax.random.uniform(key_list[2], (TOKENS, TOP), jnp.float32) ** levels(key_list[2], (TOKENS, TOP), ((0, 128),), -0.2, 0.2), 0.1, 1.0)
    experts_keys = jax.random.split(jax.random.fold_in(key_list[3], 1), TOKENS // TOK_DEV)
    experts_turns = jax.random.permutation(jax.random.fold_in(key_list[3], 3), TOKENS // TOK_DEV)
    experts = jax.vmap(lambda own, number: deal_out(jax.random.fold_in(key_list[3], 2), own, number, TOK_DEV, EXPERTS, TOP, CAP, 2))(experts_keys, experts_turns).reshape((TOKENS, TOP))
    owner = jax.random.permutation(key_list[4], EXPERTS).astype(jnp.int32)
    swapped = plant((jax.random.randint(key_list[5], (PAIRS,), 0, 2) < 1).astype(jnp.int32), jax.random.fold_in(key_list[5], 1), 0, 1)
    w_gate = bell_draw(key_list[6], (EXPERTS, D, FF), D ** -0.5, 0.125, ((0, 128),))
    w_up = bell_draw(key_list[7], (EXPERTS, D, FF), D ** -0.5, 0.125, ((0, 128),))
    w_down = bell_draw(key_list[8], (EXPERTS, FF, D), FF ** -0.5, 0.21875, ((0, 128),))
    return {"tokens": tokens, "cotangent": cotangent, "gates": gates, "experts": experts, "owner": owner, "swapped": swapped, "w_gate": w_gate, "w_up": w_up, "w_down": w_down}


def expert_rows(rows, cots, wg, wu, wd):
    act_a = jnp.dot(rows, wg, preferred_element_type=jnp.float32)
    act_b = jnp.dot(rows, wu, preferred_element_type=jnp.float32)
    sig = jax.nn.sigmoid(act_a)
    hidden = (act_a * sig * act_b).astype(jnp.bfloat16)
    out_rows = jnp.dot(hidden, wd, preferred_element_type=jnp.float32).astype(jnp.bfloat16)
    back_hidden = lax.dot_general(cots, wd, (((1,), (1,)), ((), ())), preferred_element_type=jnp.float32)
    grad_a = (back_hidden * act_b * sig * (1.0 + act_a * (1.0 - sig))).astype(jnp.bfloat16)
    grad_b = (back_hidden * act_a * sig).astype(jnp.bfloat16)
    pair_grad = lax.dot_general(grad_a, wg, (((1,), (1,)), ((), ())), preferred_element_type=jnp.float32)
    pair_grad = pair_grad + lax.dot_general(grad_b, wu, (((1,), (1,)), ((), ())), preferred_element_type=jnp.float32)
    return out_rows, pair_grad.astype(jnp.bfloat16)


def reference(tokens, cotangent, gates, experts, owner, swapped, w_gate, w_up, w_down):
    pairs = TOKENS * TOP
    slab = N_EP * CAP
    flat_e = experts.reshape(-1).astype(jnp.int32)
    planned = owner[flat_e].astype(jnp.int32)
    flag = swapped[planned // 2].astype(jnp.int32)
    target = (planned + flag * (1 - 2 * (planned % 2))).astype(jnp.int32)
    blocks = target.reshape(N_EP, TOK_DEV * TOP)
    hot = (blocks[:, :, None] == jnp.arange(N_EP, dtype=jnp.int32)[None, None, :]).astype(jnp.int32)
    running = jnp.cumsum(hot, axis=1)
    rank = (jnp.sum(hot * running, axis=2) - 1).reshape(-1)
    source_dev = jnp.arange(pairs, dtype=jnp.int32) // (TOK_DEV * TOP)
    place = target * slab + source_dev * CAP + rank
    table = jnp.full((N_EP * slab,), pairs, jnp.int32).at[place].set(jnp.arange(pairs, dtype=jnp.int32))
    tok_pad = jnp.concatenate([tokens, jnp.zeros((1, D), jnp.bfloat16)], axis=0)
    cot_pad = jnp.concatenate([cotangent, jnp.zeros((1, D), jnp.bfloat16)], axis=0)
    gate_pad = jnp.concatenate([gates.reshape(-1), jnp.zeros((1,), jnp.float32)], axis=0)

    def one_device(carry, device):
        mixed_acc, grad_acc, gate_acc = carry
        rows_idx = lax.dynamic_slice_in_dim(table, device * slab, slab)
        token_idx = rows_idx // TOP
        rows = tok_pad[token_idx]
        weight = gate_pad[rows_idx]
        dy_rows = cot_pad[token_idx].astype(jnp.float32)
        cots = (dy_rows * weight[:, None]).astype(jnp.bfloat16)
        out_rows, pair_grad = expert_rows(rows, cots, w_gate[device], w_up[device], w_down[device])
        out_f = out_rows.astype(jnp.float32)
        mixed_acc = mixed_acc.at[token_idx].add(weight[:, None] * out_f, mode="drop")
        grad_acc = grad_acc.at[token_idx].add(pair_grad.astype(jnp.float32), mode="drop")
        gate_acc = gate_acc.at[rows_idx].set(jnp.sum(dy_rows * out_f, axis=1), mode="drop")
        return (mixed_acc, grad_acc, gate_acc), None

    start = (jnp.zeros((TOKENS, D), jnp.float32), jnp.zeros((TOKENS, D), jnp.float32), jnp.zeros((pairs,), jnp.float32))
    final, _ = lax.scan(one_device, start, jnp.arange(N_EP, dtype=jnp.int32))
    mixed_acc, grad_acc, gate_acc = final
    return mixed_acc.astype(jnp.bfloat16), grad_acc.astype(jnp.bfloat16), gate_acc.reshape(TOKENS, TOP)
```

```python
import jax
import jax.numpy as jnp
from jax import lax
from jax.sharding import PartitionSpec as P

LANES = 128


def project_in(flat, wg, wu):
    act_a = jnp.dot(flat, wg, preferred_element_type=jnp.float32)
    act_b = jnp.dot(flat, wu, preferred_element_type=jnp.float32)
    return (act_a, act_b)


def project_out(act_a, act_b, wd):
    sig = jax.nn.sigmoid(act_a)
    hidden = (act_a * sig * act_b).astype(jnp.bfloat16)
    return jnp.dot(hidden, wd, preferred_element_type=jnp.float32).astype(jnp.bfloat16)


def project_back(cots, act_a, act_b, wg, wu, wd):
    sig = jax.nn.sigmoid(act_a)
    back_hidden = lax.dot_general(
        cots, wd, (((1,), (1,)), ((), ())), preferred_element_type=jnp.float32
    )
    grad_a = (back_hidden * act_b * sig * (1.0 + act_a * (1.0 - sig))).astype(jnp.bfloat16)
    grad_b = (back_hidden * act_a * sig).astype(jnp.bfloat16)
    pair_grad = lax.dot_general(
        grad_a, wg, (((1,), (1,)), ((), ())), preferred_element_type=jnp.float32
    )
    pair_grad = pair_grad + lax.dot_general(
        grad_b, wu, (((1,), (1,)), ((), ())), preferred_element_type=jnp.float32
    )
    return pair_grad.astype(jnp.bfloat16)


def body(tokens, cotangent, gates, experts, owner, swapped, w_gate, w_up, w_down):
    tok_rows, width = tokens.shape
    top_count = experts.shape[1]
    expert_total = owner.shape[0]
    count = lax.axis_size("ep")
    slots = tok_rows * top_count * 3 // (2 * expert_total)
    pairs = tok_rows * top_count
    sub = width // LANES
    devices = jnp.arange(count, dtype=jnp.int32)
    dev_flag = jnp.repeat(swapped, 2)
    step_dev = dev_flag * (1 - 2 * (devices % 2))
    holder = owner + jnp.sum(
        jnp.where(owner[:, None] == devices[None, :], step_dev[None, :], 0), axis=1
    )
    wg = w_gate[0]
    wu = w_up[0]
    wd = w_down[0]
    flat_e = experts.reshape(-1)
    chosen = flat_e[:, None] == jnp.arange(expert_total, dtype=jnp.int32)[None, :]
    target = jnp.sum(jnp.where(chosen, holder[None, :], 0), axis=1)
    hot = target[:, None] == devices[None, :]
    running = jnp.cumsum(hot.astype(jnp.int32), axis=0)
    rank = jnp.sum(jnp.where(hot, running, 0), axis=1) - 1
    place = target * slots + rank
    source = (
        jnp.full((count * slots,), pairs, jnp.int32)
        .at[place]
        .set(jnp.arange(pairs, dtype=jnp.int32))
    )
    row_of = source // top_count
    tok_pad = jnp.concatenate([tokens, jnp.zeros((1, width), jnp.bfloat16)], axis=0)
    cot_pad = jnp.concatenate([cotangent, jnp.zeros((1, width), jnp.bfloat16)], axis=0)
    gate_pad = jnp.concatenate([gates.reshape(-1), jnp.zeros((1,), jnp.float32)], axis=0)
    tok3 = tok_pad.reshape(tok_rows + 1, sub, LANES)
    cot3 = cot_pad.reshape(tok_rows + 1, sub, LANES)
    send_x = tok3[row_of].reshape(count, slots, sub, LANES)
    send_c = (cot3[row_of].astype(jnp.float32) * gate_pad[source][:, None, None]).astype(jnp.bfloat16)
    send_c = send_c.reshape(count, slots, sub, LANES)
    recv_x = lax.all_to_all(send_x, "ep", split_axis=0, concat_axis=0, tiled=True)
    recv_c = lax.all_to_all(send_c, "ep", split_axis=0, concat_axis=0, tiled=True)
    flat = recv_x.reshape(-1, width)
    act_a, act_b = project_in(flat, wg, wu)
    out_rows = project_out(act_a, act_b, wd)
    back = lax.all_to_all(
        out_rows.reshape(count, slots, sub, LANES), "ep", split_axis=0, concat_axis=0, tiled=True
    )
    pair_grad = project_back(recv_c.reshape(-1, width), act_a, act_b, wg, wu, wd)
    grad_back = lax.all_to_all(
        pair_grad.reshape(count, slots, sub, LANES), "ep", split_axis=0, concat_axis=0, tiled=True
    )
    out_pairs = (
        back.reshape(-1, sub, LANES)[place]
        .reshape(tok_rows, top_count, sub, LANES)
        .astype(jnp.float32)
    )
    grad_pairs = (
        grad_back.reshape(-1, sub, LANES)[place]
        .reshape(tok_rows, top_count, sub, LANES)
        .astype(jnp.float32)
    )
    mixed = jnp.sum(gates[:, :, None, None] * out_pairs, axis=1).astype(jnp.bfloat16)
    cot_f = cotangent.reshape(tok_rows, 1, sub, LANES).astype(jnp.float32)
    gate_grad = jnp.sum(cot_f * out_pairs, axis=(2, 3))
    in_grad = jnp.sum(grad_pairs, axis=1).astype(jnp.bfloat16)
    return (mixed.reshape(tok_rows, width), in_grad.reshape(tok_rows, width), gate_grad)


def solution(mesh):
    return jax.shard_map(
        body,
        mesh=mesh,
        in_specs=(
            P("ep", None),
            P("ep", None),
            P("ep", None),
            P("ep", None),
            P(),
            P(),
            P("ep", None, None),
            P("ep", None, None),
            P("ep", None, None),
        ),
        out_specs=(P("ep", None), P("ep", None), P("ep", None)),
        check_vma=False,
    )
```

```python
import jax
import jax.numpy as jnp
from jax import lax
from jax.sharding import PartitionSpec as P
from jax.experimental import pallas as pl
from jax.experimental.pallas import tpu as pltpu

LANES = 128


def project_in(flat, wg, wu):
    act_a = jnp.dot(flat, wg, preferred_element_type=jnp.float32)
    act_b = jnp.dot(flat, wu, preferred_element_type=jnp.float32)
    return (act_a, act_b)


def project_out(act_a, act_b, wd):
    sig = jax.nn.sigmoid(act_a)
    hidden = (act_a * sig * act_b).astype(jnp.bfloat16)
    return jnp.dot(hidden, wd, preferred_element_type=jnp.float32).astype(jnp.bfloat16)


def project_back(cots, act_a, act_b, wg, wu, wd):
    sig = jax.nn.sigmoid(act_a)
    back_hidden = lax.dot_general(
        cots, wd, (((1,), (1,)), ((), ())), preferred_element_type=jnp.float32
    )
    grad_a = (back_hidden * act_b * sig * (1.0 + act_a * (1.0 - sig))).astype(jnp.bfloat16)
    grad_b = (back_hidden * act_a * sig).astype(jnp.bfloat16)
    pair_grad = lax.dot_general(
        grad_a, wg, (((1,), (1,)), ((), ())), preferred_element_type=jnp.float32
    )
    pair_grad = pair_grad + lax.dot_general(
        grad_b, wu, (((1,), (1,)), ((), ())), preferred_element_type=jnp.float32
    )
    return pair_grad.astype(jnp.bfloat16)


def combine_rows(place, rows, tok_rows, top_count):
    def kernel(place_ref, rows_ref, out_ref):
        def one_token(t, carry):
            acc = rows_ref[place_ref[t * top_count]].astype(jnp.float32)
            for k in range(1, top_count):
                acc = acc + rows_ref[place_ref[t * top_count + k]].astype(jnp.float32)
            out_ref[t] = acc.astype(out_ref.dtype)
            return carry

        lax.fori_loop(0, tok_rows, one_token, 0, unroll=4)

    return pl.pallas_call(
        kernel,
        out_shape=jax.ShapeDtypeStruct((tok_rows,) + rows.shape[1:], jnp.bfloat16),
        in_specs=[
            pl.BlockSpec(memory_space=pltpu.SMEM),
            pl.BlockSpec(memory_space=pltpu.VMEM),
        ],
        out_specs=pl.BlockSpec(memory_space=pltpu.VMEM),
    )(place, rows)


def body(tokens, cotangent, gates, experts, owner, swapped, w_gate, w_up, w_down):
    tok_rows, width = tokens.shape
    top_count = experts.shape[1]
    expert_total = owner.shape[0]
    count = lax.axis_size("ep")
    slots = tok_rows * top_count * 3 // (2 * expert_total)
    pairs = tok_rows * top_count
    sub = width // LANES
    devices = jnp.arange(count, dtype=jnp.int32)
    dev_flag = jnp.repeat(swapped, 2)
    step_dev = dev_flag * (1 - 2 * (devices % 2))
    holder = owner + jnp.sum(
        jnp.where(owner[:, None] == devices[None, :], step_dev[None, :], 0), axis=1
    )
    wg = w_gate[0]
    wu = w_up[0]
    wd = w_down[0]
    flat_e = experts.reshape(-1)
    chosen = flat_e[:, None] == jnp.arange(expert_total, dtype=jnp.int32)[None, :]
    target = jnp.sum(jnp.where(chosen, holder[None, :], 0), axis=1)
    hot = target[:, None] == devices[None, :]
    running = jnp.cumsum(hot.astype(jnp.int32), axis=0)
    rank = jnp.sum(jnp.where(hot, running, 0), axis=1) - 1
    place = target * slots + rank
    source = (
        jnp.full((count * slots,), pairs, jnp.int32)
        .at[place]
        .set(jnp.arange(pairs, dtype=jnp.int32))
    )
    row_of = source // top_count
    tok_pad = jnp.concatenate([tokens, jnp.zeros((1, width), jnp.bfloat16)], axis=0)
    cot_pad = jnp.concatenate([cotangent, jnp.zeros((1, width), jnp.bfloat16)], axis=0)
    gate_pad = jnp.concatenate([gates.reshape(-1), jnp.zeros((1,), jnp.float32)], axis=0)
    tok3 = tok_pad.reshape(tok_rows + 1, sub, LANES)
    cot3 = cot_pad.reshape(tok_rows + 1, sub, LANES)
    send_x = tok3[row_of].reshape(count, slots, sub, LANES)
    send_c = (cot3[row_of].astype(jnp.float32) * gate_pad[source][:, None, None]).astype(jnp.bfloat16)
    send_c = send_c.reshape(count, slots, sub, LANES)
    recv_x = lax.all_to_all(send_x, "ep", split_axis=0, concat_axis=0, tiled=True)
    recv_c = lax.all_to_all(send_c, "ep", split_axis=0, concat_axis=0, tiled=True)
    flat = recv_x.reshape(-1, width)
    act_a, act_b = project_in(flat, wg, wu)
    out_rows = project_out(act_a, act_b, wd)
    back = lax.all_to_all(
        out_rows.reshape(count, slots, sub, LANES), "ep", split_axis=0, concat_axis=0, tiled=True
    )
    pair_grad = project_back(recv_c.reshape(-1, width), act_a, act_b, wg, wu, wd)
    grad_back = lax.all_to_all(
        pair_grad.reshape(count, slots, sub, LANES), "ep", split_axis=0, concat_axis=0, tiled=True
    )
    out_pairs = (
        back.reshape(-1, sub, LANES)[place]
        .reshape(tok_rows, top_count, sub, LANES)
        .astype(jnp.float32)
    )
    mixed = jnp.sum(gates[:, :, None, None] * out_pairs, axis=1).astype(jnp.bfloat16)
    cot_f = cotangent.reshape(tok_rows, 1, sub, LANES).astype(jnp.float32)
    gate_grad = jnp.sum(cot_f * out_pairs, axis=(2, 3))
    in_grad = combine_rows(place, grad_back.reshape(-1, sub, LANES), tok_rows, top_count)
    return (mixed.reshape(tok_rows, width), in_grad.reshape(tok_rows, width), gate_grad)


def solution(mesh):
    return jax.shard_map(
        body,
        mesh=mesh,
        in_specs=(
            P("ep", None),
            P("ep", None),
            P("ep", None),
            P("ep", None),
            P(),
            P(),
            P("ep", None, None),
            P("ep", None, None),
            P("ep", None, None),
        ),
        out_specs=(P("ep", None), P("ep", None), P("ep", None)),
        check_vma=False,
    )
```

```python
import jax
import jax.numpy as jnp
from jax import lax
from jax.sharding import PartitionSpec as P
from jax.experimental import pallas as pl
from jax.experimental.pallas import tpu as pltpu

LANES = 128


def project_in(flat, wg, wu):
    act_a = jnp.dot(flat, wg, preferred_element_type=jnp.float32)
    act_b = jnp.dot(flat, wu, preferred_element_type=jnp.float32)
    return (act_a, act_b)


def project_out(act_a, act_b, wd):
    sig = jax.nn.sigmoid(act_a)
    hidden = (act_a * sig * act_b).astype(jnp.bfloat16)
    return jnp.dot(hidden, wd, preferred_element_type=jnp.float32).astype(jnp.bfloat16)


def project_back(cots, act_a, act_b, wg, wu, wd):
    sig = jax.nn.sigmoid(act_a)
    back_hidden = lax.dot_general(
        cots, wd, (((1,), (1,)), ((), ())), preferred_element_type=jnp.float32
    )
    grad_a = (back_hidden * act_b * sig * (1.0 + act_a * (1.0 - sig))).astype(jnp.bfloat16)
    grad_b = (back_hidden * act_a * sig).astype(jnp.bfloat16)
    pair_grad = lax.dot_general(
        grad_a, wg, (((1,), (1,)), ((), ())), preferred_element_type=jnp.float32
    )
    pair_grad = pair_grad + lax.dot_general(
        grad_b, wu, (((1,), (1,)), ((), ())), preferred_element_type=jnp.float32
    )
    return pair_grad.astype(jnp.bfloat16)


def combine_rows(place, rows, tok_rows, top_count):
    def kernel(place_ref, rows_ref, out_ref):
        def one_token(t, carry):
            acc = rows_ref[place_ref[t * top_count]].astype(jnp.float32)
            for k in range(1, top_count):
                acc = acc + rows_ref[place_ref[t * top_count + k]].astype(jnp.float32)
            out_ref[t] = acc.astype(out_ref.dtype)
            return carry

        lax.fori_loop(0, tok_rows, one_token, 0, unroll=4)

    return pl.pallas_call(
        kernel,
        out_shape=jax.ShapeDtypeStruct((tok_rows,) + rows.shape[1:], jnp.bfloat16),
        in_specs=[
            pl.BlockSpec(memory_space=pltpu.SMEM),
            pl.BlockSpec(memory_space=pltpu.VMEM),
        ],
        out_specs=pl.BlockSpec(memory_space=pltpu.VMEM),
    )(place, rows)


def dispatch_rows(flat_e, owner, swapped, tok3, slots, count, top_count):
    pairs = flat_e.shape[0]
    total = count * slots

    def kernel(e_ref, own_ref, sw_ref, tok_ref, place_ref, out_ref, cnt_ref):
        def clear_count(d, carry):
            cnt_ref[d] = 0
            return carry

        lax.fori_loop(0, count, clear_count, 0)

        def clear_row(i, carry):
            out_ref[i] = jnp.zeros(out_ref.shape[1:], out_ref.dtype)
            return carry

        lax.fori_loop(0, total, clear_row, 0, unroll=8)

        def one_pair(p, carry):
            planned = own_ref[e_ref[p]]
            flip = sw_ref[planned // 2] * (1 - 2 * (planned % 2))
            tgt = planned + flip
            rank = cnt_ref[tgt]
            cnt_ref[tgt] = rank + 1
            spot = jnp.minimum(tgt * slots + rank, total - 1)
            place_ref[p] = spot
            out_ref[spot] = tok_ref[p // top_count]
            return carry

        lax.fori_loop(0, pairs, one_pair, 0, unroll=4)

    smem = pl.BlockSpec(memory_space=pltpu.SMEM)
    vmem = pl.BlockSpec(memory_space=pltpu.VMEM)
    return pl.pallas_call(
        kernel,
        out_shape=(
            jax.ShapeDtypeStruct((pairs,), jnp.int32),
            jax.ShapeDtypeStruct((total,) + tok3.shape[1:], tok3.dtype),
        ),
        in_specs=[smem, smem, smem, vmem],
        out_specs=(smem, vmem),
        scratch_shapes=[pltpu.SMEM((count,), jnp.int32)],
    )(flat_e, owner, swapped, tok3)


def dispatch_cots(place, gate_flat, cot3, total, top_count):
    pairs = place.shape[0]

    def kernel(place_ref, gate_ref, cot_ref, out_ref):
        def clear_row(i, carry):
            out_ref[i] = jnp.zeros(out_ref.shape[1:], out_ref.dtype)
            return carry

        lax.fori_loop(0, total, clear_row, 0, unroll=8)

        def one_pair(p, carry):
            row = cot_ref[p // top_count].astype(jnp.float32) * gate_ref[p]
            out_ref[place_ref[p]] = row.astype(out_ref.dtype)
            return carry

        lax.fori_loop(0, pairs, one_pair, 0, unroll=4)

    smem = pl.BlockSpec(memory_space=pltpu.SMEM)
    vmem = pl.BlockSpec(memory_space=pltpu.VMEM)
    return pl.pallas_call(
        kernel,
        out_shape=jax.ShapeDtypeStruct((total,) + cot3.shape[1:], cot3.dtype),
        in_specs=[smem, smem, vmem],
        out_specs=vmem,
    )(place, gate_flat, cot3)


def body(tokens, cotangent, gates, experts, owner, swapped, w_gate, w_up, w_down):
    tok_rows, width = tokens.shape
    top_count = experts.shape[1]
    expert_total = owner.shape[0]
    count = lax.axis_size("ep")
    slots = tok_rows * top_count * 3 // (2 * expert_total)
    sub = width // LANES
    wg = w_gate[0]
    wu = w_up[0]
    wd = w_down[0]
    tok3 = tokens.reshape(tok_rows, sub, LANES)
    cot3 = cotangent.reshape(tok_rows, sub, LANES)
    place, send_x = dispatch_rows(
        experts.reshape(-1), owner, swapped, tok3, slots, count, top_count
    )
    send_c = dispatch_cots(place, gates.reshape(-1), cot3, count * slots, top_count)
    send_x = send_x.reshape(count, slots, sub, LANES)
    send_c = send_c.reshape(count, slots, sub, LANES)
    recv_x = lax.all_to_all(send_x, "ep", split_axis=0, concat_axis=0, tiled=True)
    recv_c = lax.all_to_all(send_c, "ep", split_axis=0, concat_axis=0, tiled=True)
    flat = recv_x.reshape(-1, width)
    act_a, act_b = project_in(flat, wg, wu)
    out_rows = project_out(act_a, act_b, wd)
    back = lax.all_to_all(
        out_rows.reshape(count, slots, sub, LANES), "ep", split_axis=0, concat_axis=0, tiled=True
    )
    pair_grad = project_back(recv_c.reshape(-1, width), act_a, act_b, wg, wu, wd)
    grad_back = lax.all_to_all(
        pair_grad.reshape(count, slots, sub, LANES), "ep", split_axis=0, concat_axis=0, tiled=True
    )
    out_pairs = (
        back.reshape(-1, sub, LANES)[place]
        .reshape(tok_rows, top_count, sub, LANES)
        .astype(jnp.float32)
    )
    mixed = jnp.sum(gates[:, :, None, None] * out_pairs, axis=1).astype(jnp.bfloat16)
    cot_f = cot3.reshape(tok_rows, 1, sub, LANES).astype(jnp.float32)
    gate_grad = jnp.sum(cot_f * out_pairs, axis=(2, 3))
    in_grad = combine_rows(place, grad_back.reshape(-1, sub, LANES), tok_rows, top_count)
    return (mixed.reshape(tok_rows, width), in_grad.reshape(tok_rows, width), gate_grad)


def solution(mesh):
    return jax.shard_map(
        body,
        mesh=mesh,
        in_specs=(
            P("ep", None),
            P("ep", None),
            P("ep", None),
            P("ep", None),
            P(),
            P(),
            P("ep", None, None),
            P("ep", None, None),
            P("ep", None, None),
        ),
        out_specs=(P("ep", None), P("ep", None), P("ep", None)),
        check_vma=False,
    )
```

```python
import jax
import jax.numpy as jnp
from jax import lax
from jax.sharding import PartitionSpec as P
from jax.experimental import pallas as pl
from jax.experimental.pallas import tpu as pltpu

LANES = 128


def project_in(flat, wg, wu):
    act_a = jnp.dot(flat, wg, preferred_element_type=jnp.float32)
    act_b = jnp.dot(flat, wu, preferred_element_type=jnp.float32)
    return (act_a, act_b)


def project_out(act_a, act_b, wd):
    sig = jax.nn.sigmoid(act_a)
    hidden = (act_a * sig * act_b).astype(jnp.bfloat16)
    return jnp.dot(hidden, wd, preferred_element_type=jnp.float32).astype(jnp.bfloat16)


def project_back(cots, act_a, act_b, wg, wu, wd):
    sig = jax.nn.sigmoid(act_a)
    back_hidden = lax.dot_general(
        cots, wd, (((1,), (1,)), ((), ())), preferred_element_type=jnp.float32
    )
    grad_a = (back_hidden * act_b * sig * (1.0 + act_a * (1.0 - sig))).astype(jnp.bfloat16)
    grad_b = (back_hidden * act_a * sig).astype(jnp.bfloat16)
    pair_grad = lax.dot_general(
        grad_a, wg, (((1,), (1,)), ((), ())), preferred_element_type=jnp.float32
    )
    pair_grad = pair_grad + lax.dot_general(
        grad_b, wu, (((1,), (1,)), ((), ())), preferred_element_type=jnp.float32
    )
    return pair_grad.astype(jnp.bfloat16)


def combine_rows(place, rows, tok_rows, top_count):
    def kernel(place_ref, rows_ref, out_ref):
        def one_token(t, carry):
            acc = rows_ref[place_ref[t * top_count]].astype(jnp.float32)
            for k in range(1, top_count):
                acc = acc + rows_ref[place_ref[t * top_count + k]].astype(jnp.float32)
            out_ref[t] = acc.astype(out_ref.dtype)
            return carry

        lax.fori_loop(0, tok_rows, one_token, 0, unroll=4)

    return pl.pallas_call(
        kernel,
        out_shape=jax.ShapeDtypeStruct((tok_rows,) + rows.shape[1:], jnp.bfloat16),
        in_specs=[
            pl.BlockSpec(memory_space=pltpu.SMEM),
            pl.BlockSpec(memory_space=pltpu.VMEM),
        ],
        out_specs=pl.BlockSpec(memory_space=pltpu.VMEM),
    )(place, rows)


def body(tokens, cotangent, gates, experts, owner, swapped, w_gate, w_up, w_down):
    tok_rows, width = tokens.shape
    top_count = experts.shape[1]
    expert_total = owner.shape[0]
    count = lax.axis_size("ep")
    slots = tok_rows * top_count * 3 // (2 * expert_total)
    pairs = tok_rows * top_count
    sub = width // LANES
    devices = jnp.arange(count, dtype=jnp.int32)
    dev_flag = jnp.repeat(swapped, 2)
    step_dev = dev_flag * (1 - 2 * (devices % 2))
    holder = owner + jnp.sum(
        jnp.where(owner[:, None] == devices[None, :], step_dev[None, :], 0), axis=1
    )
    wg = w_gate[0]
    wu = w_up[0]
    wd = w_down[0]
    flat_e = experts.reshape(-1)
    chosen = flat_e[:, None] == jnp.arange(expert_total, dtype=jnp.int32)[None, :]
    target = jnp.sum(jnp.where(chosen, holder[None, :], 0), axis=1)
    hot = target[:, None] == devices[None, :]
    running = jnp.cumsum(hot.astype(jnp.int32), axis=0)
    rank = jnp.sum(jnp.where(hot, running, 0), axis=1) - 1
    place = target * slots + rank
    pair_row = jnp.arange(pairs, dtype=jnp.int32) // top_count
    tok3 = tokens.reshape(tok_rows, sub, LANES)
    cot3 = cotangent.reshape(tok_rows, sub, LANES)
    empty = jnp.zeros((count * slots, sub, LANES), jnp.bfloat16)
    send_x = empty.at[place].set(tok3[pair_row], unique_indices=True)
    scaled = (cot3[pair_row].astype(jnp.float32) * gates.reshape(-1)[:, None, None]).astype(
        jnp.bfloat16
    )
    send_c = empty.at[place].set(scaled, unique_indices=True)
    send_x = send_x.reshape(count, slots, sub, LANES)
    send_c = send_c.reshape(count, slots, sub, LANES)
    recv_x = lax.all_to_all(send_x, "ep", split_axis=0, concat_axis=0, tiled=True)
    recv_c = lax.all_to_all(send_c, "ep", split_axis=0, concat_axis=0, tiled=True)
    flat = recv_x.reshape(-1, width)
    act_a, act_b = project_in(flat, wg, wu)
    out_rows = project_out(act_a, act_b, wd)
    back = lax.all_to_all(
        out_rows.reshape(count, slots, sub, LANES), "ep", split_axis=0, concat_axis=0, tiled=True
    )
    pair_grad = project_back(recv_c.reshape(-1, width), act_a, act_b, wg, wu, wd)
    grad_back = lax.all_to_all(
        pair_grad.reshape(count, slots, sub, LANES), "ep", split_axis=0, concat_axis=0, tiled=True
    )
    out_pairs = (
        back.reshape(-1, sub, LANES)[place]
        .reshape(tok_rows, top_count, sub, LANES)
        .astype(jnp.float32)
    )
    mixed = jnp.sum(gates[:, :, None, None] * out_pairs, axis=1).astype(jnp.bfloat16)
    cot_f = cot3.reshape(tok_rows, 1, sub, LANES).astype(jnp.float32)
    gate_grad = jnp.sum(cot_f * out_pairs, axis=(2, 3))
    in_grad = combine_rows(place, grad_back.reshape(-1, sub, LANES), tok_rows, top_count)
    return (mixed.reshape(tok_rows, width), in_grad.reshape(tok_rows, width), gate_grad)


def solution(mesh):
    return jax.shard_map(
        body,
        mesh=mesh,
        in_specs=(
            P("ep", None),
            P("ep", None),
            P("ep", None),
            P("ep", None),
            P(),
            P(),
            P("ep", None, None),
            P("ep", None, None),
            P("ep", None, None),
        ),
        out_specs=(P("ep", None), P("ep", None), P("ep", None)),
        check_vma=False,
    )
```

```python
import jax
import jax.numpy as jnp
from jax import lax
from jax.sharding import PartitionSpec as P
from jax.experimental import pallas as pl
from jax.experimental.pallas import tpu as pltpu

LANES = 128


def project_in(flat, wg, wu):
    act_a = jnp.dot(flat, wg, preferred_element_type=jnp.float32)
    act_b = jnp.dot(flat, wu, preferred_element_type=jnp.float32)
    return (act_a, act_b)


def project_out(act_a, act_b, wd):
    sig = jax.nn.sigmoid(act_a)
    hidden = (act_a * sig * act_b).astype(jnp.bfloat16)
    return jnp.dot(hidden, wd, preferred_element_type=jnp.float32).astype(jnp.bfloat16)


def project_back(cots, act_a, act_b, wg, wu, wd):
    sig = jax.nn.sigmoid(act_a)
    back_hidden = lax.dot_general(
        cots, wd, (((1,), (1,)), ((), ())), preferred_element_type=jnp.float32
    )
    grad_a = (back_hidden * act_b * sig * (1.0 + act_a * (1.0 - sig))).astype(jnp.bfloat16)
    grad_b = (back_hidden * act_a * sig).astype(jnp.bfloat16)
    pair_grad = lax.dot_general(
        grad_a, wg, (((1,), (1,)), ((), ())), preferred_element_type=jnp.float32
    )
    pair_grad = pair_grad + lax.dot_general(
        grad_b, wu, (((1,), (1,)), ((), ())), preferred_element_type=jnp.float32
    )
    return pair_grad.astype(jnp.bfloat16)


def combine_rows(place, rows, tok_rows, top_count):
    def kernel(place_ref, rows_ref, out_ref):
        def one_token(t, carry):
            acc = rows_ref[place_ref[t * top_count]].astype(jnp.float32)
            for k in range(1, top_count):
                acc = acc + rows_ref[place_ref[t * top_count + k]].astype(jnp.float32)
            out_ref[t] = acc.astype(out_ref.dtype)
            return carry

        lax.fori_loop(0, tok_rows, one_token, 0, unroll=4)

    return pl.pallas_call(
        kernel,
        out_shape=jax.ShapeDtypeStruct((tok_rows,) + rows.shape[1:], jnp.bfloat16),
        in_specs=[
            pl.BlockSpec(memory_space=pltpu.SMEM),
            pl.BlockSpec(memory_space=pltpu.VMEM),
        ],
        out_specs=pl.BlockSpec(memory_space=pltpu.VMEM),
    )(place, rows)


def dispatch_tiles(place, gate_flat, src3, total, top_count):
    pairs = place.shape[0]

    def kernel(place_ref, *refs):
        if gate_flat is None:
            src_ref, out_ref = refs
        else:
            gate_ref, src_ref, out_ref = refs

        def clear_row(i, carry):
            out_ref[i] = jnp.zeros(out_ref.shape[1:], out_ref.dtype)
            return carry

        lax.fori_loop(0, total, clear_row, 0, unroll=8)

        def one_pair(p, carry):
            if gate_flat is None:
                out_ref[place_ref[p]] = src_ref[p // top_count]
            else:
                row = src_ref[p // top_count].astype(jnp.float32) * gate_ref[p]
                out_ref[place_ref[p]] = row.astype(out_ref.dtype)
            return carry

        lax.fori_loop(0, pairs, one_pair, 0, unroll=4)

    smem = pl.BlockSpec(memory_space=pltpu.SMEM)
    vmem = pl.BlockSpec(memory_space=pltpu.VMEM)
    return pl.pallas_call(
        kernel,
        out_shape=jax.ShapeDtypeStruct((total,) + src3.shape[1:], src3.dtype),
        in_specs=[smem, vmem] if gate_flat is None else [smem, smem, vmem],
        out_specs=vmem,
    )(*((place, src3) if gate_flat is None else (place, gate_flat, src3)))


def body(tokens, cotangent, gates, experts, owner, swapped, w_gate, w_up, w_down):
    tok_rows, width = tokens.shape
    top_count = experts.shape[1]
    expert_total = owner.shape[0]
    count = lax.axis_size("ep")
    slots = tok_rows * top_count * 3 // (2 * expert_total)
    pairs = tok_rows * top_count
    sub = width // LANES
    devices = jnp.arange(count, dtype=jnp.int32)
    dev_flag = jnp.repeat(swapped, 2)
    step_dev = dev_flag * (1 - 2 * (devices % 2))
    holder = owner + jnp.sum(
        jnp.where(owner[:, None] == devices[None, :], step_dev[None, :], 0), axis=1
    )
    wg = w_gate[0]
    wu = w_up[0]
    wd = w_down[0]
    flat_e = experts.reshape(-1)
    chosen = flat_e[:, None] == jnp.arange(expert_total, dtype=jnp.int32)[None, :]
    target = jnp.sum(jnp.where(chosen, holder[None, :], 0), axis=1)
    hot = target[:, None] == devices[None, :]
    running = jnp.cumsum(hot.astype(jnp.int32), axis=0)
    rank = jnp.sum(jnp.where(hot, running, 0), axis=1) - 1
    place = target * slots + rank
    tok3 = tokens.reshape(tok_rows, sub, LANES)
    cot3 = cotangent.reshape(tok_rows, sub, LANES)
    send_x = dispatch_tiles(place, None, tok3, count * slots, top_count)
    send_c = dispatch_tiles(place, gates.reshape(-1), cot3, count * slots, top_count)
    send_x = send_x.reshape(count, slots, sub, LANES)
    send_c = send_c.reshape(count, slots, sub, LANES)
    recv_x = lax.all_to_all(send_x, "ep", split_axis=0, concat_axis=0, tiled=True)
    recv_c = lax.all_to_all(send_c, "ep", split_axis=0, concat_axis=0, tiled=True)
    flat = recv_x.reshape(-1, width)
    act_a, act_b = project_in(flat, wg, wu)
    out_rows = project_out(act_a, act_b, wd)
    back = lax.all_to_all(
        out_rows.reshape(count, slots, sub, LANES), "ep", split_axis=0, concat_axis=0, tiled=True
    )
    pair_grad = project_back(recv_c.reshape(-1, width), act_a, act_b, wg, wu, wd)
    grad_back = lax.all_to_all(
        pair_grad.reshape(count, slots, sub, LANES), "ep", split_axis=0, concat_axis=0, tiled=True
    )
    out_pairs = (
        back.reshape(-1, sub, LANES)[place]
        .reshape(tok_rows, top_count, sub, LANES)
        .astype(jnp.float32)
    )
    mixed = jnp.sum(gates[:, :, None, None] * out_pairs, axis=1).astype(jnp.bfloat16)
    cot_f = cot3.reshape(tok_rows, 1, sub, LANES).astype(jnp.float32)
    gate_grad = jnp.sum(cot_f * out_pairs, axis=(2, 3))
    in_grad = combine_rows(place, grad_back.reshape(-1, sub, LANES), tok_rows, top_count)
    return (mixed.reshape(tok_rows, width), in_grad.reshape(tok_rows, width), gate_grad)


def solution(mesh):
    return jax.shard_map(
        body,
        mesh=mesh,
        in_specs=(
            P("ep", None),
            P("ep", None),
            P("ep", None),
            P("ep", None),
            P(),
            P(),
            P("ep", None, None),
            P("ep", None, None),
            P("ep", None, None),
        ),
        out_specs=(P("ep", None), P("ep", None), P("ep", None)),
        check_vma=False,
    )
```

```python
import jax
import jax.numpy as jnp
from jax import lax
from jax.sharding import PartitionSpec as P
from jax.experimental import pallas as pl
from jax.experimental.pallas import tpu as pltpu

LANES = 128


def project_in(flat, wg, wu):
    act_a = jnp.dot(flat, wg, preferred_element_type=jnp.float32)
    act_b = jnp.dot(flat, wu, preferred_element_type=jnp.float32)
    return (act_a, act_b)


def project_out(act_a, act_b, wd):
    sig = jax.nn.sigmoid(act_a)
    hidden = (act_a * sig * act_b).astype(jnp.bfloat16)
    return jnp.dot(hidden, wd, preferred_element_type=jnp.float32).astype(jnp.bfloat16)


def project_back(cots, act_a, act_b, wg, wu, wd):
    sig = jax.nn.sigmoid(act_a)
    back_hidden = lax.dot_general(
        cots, wd, (((1,), (1,)), ((), ())), preferred_element_type=jnp.float32
    )
    grad_a = (back_hidden * act_b * sig * (1.0 + act_a * (1.0 - sig))).astype(jnp.bfloat16)
    grad_b = (back_hidden * act_a * sig).astype(jnp.bfloat16)
    pair_grad = lax.dot_general(
        grad_a, wg, (((1,), (1,)), ((), ())), preferred_element_type=jnp.float32
    )
    pair_grad = pair_grad + lax.dot_general(
        grad_b, wu, (((1,), (1,)), ((), ())), preferred_element_type=jnp.float32
    )
    return pair_grad.astype(jnp.bfloat16)


def combine_rows(place, rows, tok_rows, top_count):
    def kernel(place_ref, rows_ref, out_ref):
        def one_token(t, carry):
            acc = rows_ref[place_ref[t * top_count]].astype(jnp.float32)
            for k in range(1, top_count):
                acc = acc + rows_ref[place_ref[t * top_count + k]].astype(jnp.float32)
            out_ref[t] = acc.astype(out_ref.dtype)
            return carry

        lax.fori_loop(0, tok_rows, one_token, 0, unroll=4)

    return pl.pallas_call(
        kernel,
        out_shape=jax.ShapeDtypeStruct((tok_rows,) + rows.shape[1:], jnp.bfloat16),
        in_specs=[
            pl.BlockSpec(memory_space=pltpu.SMEM),
            pl.BlockSpec(memory_space=pltpu.VMEM),
        ],
        out_specs=pl.BlockSpec(memory_space=pltpu.VMEM),
    )(place, rows)


def body(tokens, cotangent, gates, experts, owner, swapped, w_gate, w_up, w_down):
    tok_rows, width = tokens.shape
    top_count = experts.shape[1]
    expert_total = owner.shape[0]
    count = lax.axis_size("ep")
    slots = tok_rows * top_count * 3 // (2 * expert_total)
    pairs = tok_rows * top_count
    sub = width // LANES
    devices = jnp.arange(count, dtype=jnp.int32)
    dev_flag = jnp.repeat(swapped, 2)
    step_dev = dev_flag * (1 - 2 * (devices % 2))
    holder = owner + jnp.sum(
        jnp.where(owner[:, None] == devices[None, :], step_dev[None, :], 0), axis=1
    )
    wg = w_gate[0]
    wu = w_up[0]
    wd = w_down[0]
    flat_e = experts.reshape(-1)
    chosen = flat_e[:, None] == jnp.arange(expert_total, dtype=jnp.int32)[None, :]
    target = jnp.sum(jnp.where(chosen, holder[None, :], 0), axis=1)
    hot = target[:, None] == devices[None, :]
    running = jnp.cumsum(hot.astype(jnp.int32), axis=0)
    rank = jnp.sum(jnp.where(hot, running, 0), axis=1) - 1
    place = target * slots + rank
    slot_ids = jnp.arange(count * slots, dtype=jnp.int32)
    pair_ids = jnp.arange(pairs, dtype=jnp.int32)
    source = jnp.min(
        jnp.where(place[None, :] == slot_ids[:, None], pair_ids[None, :], pairs), axis=1
    )
    row_of = source // top_count
    tok_pad = jnp.concatenate([tokens, jnp.zeros((1, width), jnp.bfloat16)], axis=0)
    cot_pad = jnp.concatenate([cotangent, jnp.zeros((1, width), jnp.bfloat16)], axis=0)
    gate_pad = jnp.concatenate([gates.reshape(-1), jnp.zeros((1,), jnp.float32)], axis=0)
    tok3 = tok_pad.reshape(tok_rows + 1, sub, LANES)
    cot3 = cot_pad.reshape(tok_rows + 1, sub, LANES)
    send_x = tok3[row_of].reshape(count, slots, sub, LANES)
    send_c = (cot3[row_of].astype(jnp.float32) * gate_pad[source][:, None, None]).astype(jnp.bfloat16)
    send_c = send_c.reshape(count, slots, sub, LANES)
    recv_x = lax.all_to_all(send_x, "ep", split_axis=0, concat_axis=0, tiled=True)
    recv_c = lax.all_to_all(send_c, "ep", split_axis=0, concat_axis=0, tiled=True)
    flat = recv_x.reshape(-1, width)
    act_a, act_b = project_in(flat, wg, wu)
    out_rows = project_out(act_a, act_b, wd)
    back = lax.all_to_all(
        out_rows.reshape(count, slots, sub, LANES), "ep", split_axis=0, concat_axis=0, tiled=True
    )
    pair_grad = project_back(recv_c.reshape(-1, width), act_a, act_b, wg, wu, wd)
    grad_back = lax.all_to_all(
        pair_grad.reshape(count, slots, sub, LANES), "ep", split_axis=0, concat_axis=0, tiled=True
    )
    out_pairs = (
        back.reshape(-1, sub, LANES)[place]
        .reshape(tok_rows, top_count, sub, LANES)
        .astype(jnp.float32)
    )
    mixed = jnp.sum(gates[:, :, None, None] * out_pairs, axis=1).astype(jnp.bfloat16)
    cot_f = cotangent.reshape(tok_rows, 1, sub, LANES).astype(jnp.float32)
    gate_grad = jnp.sum(cot_f * out_pairs, axis=(2, 3))
    in_grad = combine_rows(place, grad_back.reshape(-1, sub, LANES), tok_rows, top_count)
    return (mixed.reshape(tok_rows, width), in_grad.reshape(tok_rows, width), gate_grad)


def solution(mesh):
    return jax.shard_map(
        body,
        mesh=mesh,
        in_specs=(
            P("ep", None),
            P("ep", None),
            P("ep", None),
            P("ep", None),
            P(),
            P(),
            P("ep", None, None),
            P("ep", None, None),
            P("ep", None, None),
        ),
        out_specs=(P("ep", None), P("ep", None), P("ep", None)),
        check_vma=False,
    )
```

```python
import jax
import jax.numpy as jnp
from jax import lax
from jax.sharding import PartitionSpec as P
from jax.experimental import pallas as pl
from jax.experimental.pallas import tpu as pltpu

LANES = 128


def project_in(flat, wg, wu):
    act_a = jnp.dot(flat, wg, preferred_element_type=jnp.float32)
    act_b = jnp.dot(flat, wu, preferred_element_type=jnp.float32)
    return (act_a, act_b)


def project_out(act_a, act_b, wd):
    sig = jax.nn.sigmoid(act_a)
    hidden = (act_a * sig * act_b).astype(jnp.bfloat16)
    return jnp.dot(hidden, wd, preferred_element_type=jnp.float32).astype(jnp.bfloat16)


def project_back(cots, act_a, act_b, wg, wu, wd):
    sig = jax.nn.sigmoid(act_a)
    back_hidden = lax.dot_general(
        cots, wd, (((1,), (1,)), ((), ())), preferred_element_type=jnp.float32
    )
    grad_a = (back_hidden * act_b * sig * (1.0 + act_a * (1.0 - sig))).astype(jnp.bfloat16)
    grad_b = (back_hidden * act_a * sig).astype(jnp.bfloat16)
    pair_grad = lax.dot_general(
        grad_a, wg, (((1,), (1,)), ((), ())), preferred_element_type=jnp.float32
    )
    pair_grad = pair_grad + lax.dot_general(
        grad_b, wu, (((1,), (1,)), ((), ())), preferred_element_type=jnp.float32
    )
    return pair_grad.astype(jnp.bfloat16)


def combine_rows(place, rows, tok_rows, top_count):
    def kernel(place_ref, rows_ref, out_ref):
        def one_token(t, carry):
            acc = rows_ref[place_ref[t * top_count]].astype(jnp.float32)
            for k in range(1, top_count):
                acc = acc + rows_ref[place_ref[t * top_count + k]].astype(jnp.float32)
            out_ref[t] = acc.astype(out_ref.dtype)
            return carry

        lax.fori_loop(0, tok_rows, one_token, 0, unroll=4)

    return pl.pallas_call(
        kernel,
        out_shape=jax.ShapeDtypeStruct((tok_rows,) + rows.shape[1:], jnp.bfloat16),
        in_specs=[
            pl.BlockSpec(memory_space=pltpu.SMEM),
            pl.BlockSpec(memory_space=pltpu.VMEM),
        ],
        out_specs=pl.BlockSpec(memory_space=pltpu.VMEM),
    )(place, rows)


def body(tokens, cotangent, gates, experts, owner, swapped, w_gate, w_up, w_down):
    tok_rows, width = tokens.shape
    top_count = experts.shape[1]
    expert_total = owner.shape[0]
    count = lax.axis_size("ep")
    slots = tok_rows * top_count * 3 // (2 * expert_total)
    pairs = tok_rows * top_count
    sub = width // LANES
    pair_slots = jnp.arange(swapped.shape[0], dtype=jnp.int32)
    flag = jnp.sum(
        jnp.where((owner // 2)[:, None] == pair_slots[None, :], swapped[None, :], 0), axis=1
    )
    holder = owner + flag * (1 - 2 * (owner % 2))
    wg = w_gate[0]
    wu = w_up[0]
    wd = w_down[0]
    flat_e = experts.reshape(-1)
    chosen = flat_e[:, None] == jnp.arange(expert_total, dtype=jnp.int32)[None, :]
    target = jnp.sum(jnp.where(chosen, holder[None, :], 0), axis=1)
    pair_ids = jnp.arange(pairs, dtype=jnp.int32)
    earlier = (target[None, :] == target[:, None]) & (pair_ids[None, :] < pair_ids[:, None])
    rank = jnp.sum(earlier.astype(jnp.int32), axis=1)
    place = target * slots + rank
    slot_ids = jnp.arange(count * slots, dtype=jnp.int32)
    source = jnp.min(
        jnp.where(place[None, :] == slot_ids[:, None], pair_ids[None, :], pairs), axis=1
    )
    row_of = source // top_count
    tok_pad = jnp.concatenate([tokens, jnp.zeros((1, width), jnp.bfloat16)], axis=0)
    cot_pad = jnp.concatenate([cotangent, jnp.zeros((1, width), jnp.bfloat16)], axis=0)
    gate_pad = jnp.concatenate([gates.reshape(-1), jnp.zeros((1,), jnp.float32)], axis=0)
    tok3 = tok_pad.reshape(tok_rows + 1, sub, LANES)
    cot3 = cot_pad.reshape(tok_rows + 1, sub, LANES)
    send_x = tok3[row_of].reshape(count, slots, sub, LANES)
    send_c = (cot3[row_of].astype(jnp.float32) * gate_pad[source][:, None, None]).astype(jnp.bfloat16)
    send_c = send_c.reshape(count, slots, sub, LANES)
    recv_x = lax.all_to_all(send_x, "ep", split_axis=0, concat_axis=0, tiled=True)
    recv_c = lax.all_to_all(send_c, "ep", split_axis=0, concat_axis=0, tiled=True)
    flat = recv_x.reshape(-1, width)
    act_a, act_b = project_in(flat, wg, wu)
    out_rows = project_out(act_a, act_b, wd)
    back = lax.all_to_all(
        out_rows.reshape(count, slots, sub, LANES), "ep", split_axis=0, concat_axis=0, tiled=True
    )
    pair_grad = project_back(recv_c.reshape(-1, width), act_a, act_b, wg, wu, wd)
    grad_back = lax.all_to_all(
        pair_grad.reshape(count, slots, sub, LANES), "ep", split_axis=0, concat_axis=0, tiled=True
    )
    out_pairs = (
        back.reshape(-1, sub, LANES)[place]
        .reshape(tok_rows, top_count, sub, LANES)
        .astype(jnp.float32)
    )
    mixed = jnp.sum(gates[:, :, None, None] * out_pairs, axis=1).astype(jnp.bfloat16)
    cot_f = cotangent.reshape(tok_rows, 1, sub, LANES).astype(jnp.float32)
    gate_grad = jnp.sum(cot_f * out_pairs, axis=(2, 3))
    in_grad = combine_rows(place, grad_back.reshape(-1, sub, LANES), tok_rows, top_count)
    return (mixed.reshape(tok_rows, width), in_grad.reshape(tok_rows, width), gate_grad)


def solution(mesh):
    return jax.shard_map(
        body,
        mesh=mesh,
        in_specs=(
            P("ep", None),
            P("ep", None),
            P("ep", None),
            P("ep", None),
            P(),
            P(),
            P("ep", None, None),
            P("ep", None, None),
            P("ep", None, None),
        ),
        out_specs=(P("ep", None), P("ep", None), P("ep", None)),
        check_vma=False,
    )
```

```python
import jax
import jax.numpy as jnp
from jax import lax
from jax.sharding import PartitionSpec as P
from jax.experimental import pallas as pl
from jax.experimental.pallas import tpu as pltpu

LANES = 128


def project_in(flat, wg, wu):
    act_a = jnp.dot(flat, wg, preferred_element_type=jnp.float32)
    act_b = jnp.dot(flat, wu, preferred_element_type=jnp.float32)
    return (act_a, act_b)


def project_out(act_a, act_b, wd):
    sig = jax.nn.sigmoid(act_a)
    hidden = (act_a * sig * act_b).astype(jnp.bfloat16)
    return jnp.dot(hidden, wd, preferred_element_type=jnp.float32).astype(jnp.bfloat16)


def project_back(cots, act_a, act_b, wg, wu, wd):
    sig = jax.nn.sigmoid(act_a)
    back_hidden = lax.dot_general(
        cots, wd, (((1,), (1,)), ((), ())), preferred_element_type=jnp.float32
    )
    grad_a = (back_hidden * act_b * sig * (1.0 + act_a * (1.0 - sig))).astype(jnp.bfloat16)
    grad_b = (back_hidden * act_a * sig).astype(jnp.bfloat16)
    pair_grad = lax.dot_general(
        grad_a, wg, (((1,), (1,)), ((), ())), preferred_element_type=jnp.float32
    )
    pair_grad = pair_grad + lax.dot_general(
        grad_b, wu, (((1,), (1,)), ((), ())), preferred_element_type=jnp.float32
    )
    return pair_grad.astype(jnp.bfloat16)


def combine_rows(place, rows, tok_rows, top_count):
    def kernel(place_ref, rows_ref, out_ref):
        def one_token(t, carry):
            acc = rows_ref[place_ref[t * top_count]].astype(jnp.float32)
            for k in range(1, top_count):
                acc = acc + rows_ref[place_ref[t * top_count + k]].astype(jnp.float32)
            out_ref[t] = acc.astype(out_ref.dtype)
            return carry

        lax.fori_loop(0, tok_rows, one_token, 0, unroll=4)

    return pl.pallas_call(
        kernel,
        out_shape=jax.ShapeDtypeStruct((tok_rows,) + rows.shape[1:], jnp.bfloat16),
        in_specs=[
            pl.BlockSpec(memory_space=pltpu.SMEM),
            pl.BlockSpec(memory_space=pltpu.VMEM),
        ],
        out_specs=pl.BlockSpec(memory_space=pltpu.VMEM),
    )(place, rows)


def gather_tiles(row_of, src3, block):
    total = row_of.shape[0]

    def kernel(row_ref, src_ref, out_ref):
        base = pl.program_id(0) * block

        def one_slot(i, carry):
            out_ref[i] = src_ref[row_ref[base + i]]
            return carry

        lax.fori_loop(0, block, one_slot, 0, unroll=8)

    return pl.pallas_call(
        kernel,
        out_shape=jax.ShapeDtypeStruct((total,) + src3.shape[1:], src3.dtype),
        grid_spec=pltpu.PrefetchScalarGridSpec(
            num_scalar_prefetch=1,
            grid=(total // block,),
            in_specs=[pl.BlockSpec(src3.shape, lambda g, rows: (0, 0, 0))],
            out_specs=pl.BlockSpec((block,) + src3.shape[1:], lambda g, rows: (g, 0, 0)),
        ),
    )(row_of, src3)


def body(tokens, cotangent, gates, experts, owner, swapped, w_gate, w_up, w_down):
    tok_rows, width = tokens.shape
    top_count = experts.shape[1]
    expert_total = owner.shape[0]
    count = lax.axis_size("ep")
    slots = tok_rows * top_count * 3 // (2 * expert_total)
    pairs = tok_rows * top_count
    sub = width // LANES
    pair_slots = jnp.arange(swapped.shape[0], dtype=jnp.int32)
    flag = jnp.sum(
        jnp.where((owner // 2)[:, None] == pair_slots[None, :], swapped[None, :], 0), axis=1
    )
    holder = owner + flag * (1 - 2 * (owner % 2))
    wg = w_gate[0]
    wu = w_up[0]
    wd = w_down[0]
    flat_e = experts.reshape(-1)
    chosen = flat_e[:, None] == jnp.arange(expert_total, dtype=jnp.int32)[None, :]
    target = jnp.sum(jnp.where(chosen, holder[None, :], 0), axis=1)
    pair_ids = jnp.arange(pairs, dtype=jnp.int32)
    earlier = (target[None, :] == target[:, None]) & (pair_ids[None, :] < pair_ids[:, None])
    rank = jnp.sum(earlier.astype(jnp.int32), axis=1)
    place = target * slots + rank
    slot_ids = jnp.arange(count * slots, dtype=jnp.int32)
    source = jnp.min(
        jnp.where(place[None, :] == slot_ids[:, None], pair_ids[None, :], pairs), axis=1
    )
    row_of = source // top_count
    tok_pad = jnp.concatenate([tokens, jnp.zeros((1, width), jnp.bfloat16)], axis=0)
    cot_pad = jnp.concatenate([cotangent, jnp.zeros((1, width), jnp.bfloat16)], axis=0)
    gate_pad = jnp.concatenate([gates.reshape(-1), jnp.zeros((1,), jnp.float32)], axis=0)
    tok3 = tok_pad.reshape(tok_rows + 1, sub, LANES)
    cot3 = cot_pad.reshape(tok_rows + 1, sub, LANES)
    send_x = gather_tiles(
        jnp.minimum(row_of, tok_rows - 1), tokens.reshape(tok_rows, sub, LANES), 256
    ).reshape(count, slots, sub, LANES)
    send_c = (cot3[row_of].astype(jnp.float32) * gate_pad[source][:, None, None]).astype(jnp.bfloat16)
    send_c = send_c.reshape(count, slots, sub, LANES)
    recv_x = lax.all_to_all(send_x, "ep", split_axis=0, concat_axis=0, tiled=True)
    recv_c = lax.all_to_all(send_c, "ep", split_axis=0, concat_axis=0, tiled=True)
    flat = recv_x.reshape(-1, width)
    act_a, act_b = project_in(flat, wg, wu)
    out_rows = project_out(act_a, act_b, wd)
    back = lax.all_to_all(
        out_rows.reshape(count, slots, sub, LANES), "ep", split_axis=0, concat_axis=0, tiled=True
    )
    pair_grad = project_back(recv_c.reshape(-1, width), act_a, act_b, wg, wu, wd)
    grad_back = lax.all_to_all(
        pair_grad.reshape(count, slots, sub, LANES), "ep", split_axis=0, concat_axis=0, tiled=True
    )
    out_pairs = (
        back.reshape(-1, sub, LANES)[place]
        .reshape(tok_rows, top_count, sub, LANES)
        .astype(jnp.float32)
    )
    mixed = jnp.sum(gates[:, :, None, None] * out_pairs, axis=1).astype(jnp.bfloat16)
    cot_f = cotangent.reshape(tok_rows, 1, sub, LANES).astype(jnp.float32)
    gate_grad = jnp.sum(cot_f * out_pairs, axis=(2, 3))
    in_grad = combine_rows(place, grad_back.reshape(-1, sub, LANES), tok_rows, top_count)
    return (mixed.reshape(tok_rows, width), in_grad.reshape(tok_rows, width), gate_grad)


def solution(mesh):
    return jax.shard_map(
        body,
        mesh=mesh,
        in_specs=(
            P("ep", None),
            P("ep", None),
            P("ep", None),
            P("ep", None),
            P(),
            P(),
            P("ep", None, None),
            P("ep", None, None),
            P("ep", None, None),
        ),
        out_specs=(P("ep", None), P("ep", None), P("ep", None)),
        check_vma=False,
    )
```

```python
import jax
import jax.numpy as jnp
from jax import lax
from jax.sharding import PartitionSpec as P
from jax.experimental import pallas as pl
from jax.experimental.pallas import tpu as pltpu

LANES = 128


def project_in(flat, wg, wu):
    act_a = jnp.dot(flat, wg, preferred_element_type=jnp.float32)
    act_b = jnp.dot(flat, wu, preferred_element_type=jnp.float32)
    return (act_a, act_b)


def project_out(act_a, act_b, wd):
    sig = jax.nn.sigmoid(act_a)
    hidden = (act_a * sig * act_b).astype(jnp.bfloat16)
    return jnp.dot(hidden, wd, preferred_element_type=jnp.float32).astype(jnp.bfloat16)


def project_back(cots, act_a, act_b, wg, wu, wd):
    sig = jax.nn.sigmoid(act_a)
    back_hidden = lax.dot_general(
        cots, wd, (((1,), (1,)), ((), ())), preferred_element_type=jnp.float32
    )
    grad_a = (back_hidden * act_b * sig * (1.0 + act_a * (1.0 - sig))).astype(jnp.bfloat16)
    grad_b = (back_hidden * act_a * sig).astype(jnp.bfloat16)
    pair_grad = lax.dot_general(
        grad_a, wg, (((1,), (1,)), ((), ())), preferred_element_type=jnp.float32
    )
    pair_grad = pair_grad + lax.dot_general(
        grad_b, wu, (((1,), (1,)), ((), ())), preferred_element_type=jnp.float32
    )
    return pair_grad.astype(jnp.bfloat16)


def combine_rows(place, rows, tok_rows, top_count):
    def kernel(place_ref, rows_ref, out_ref):
        def one_token(t, carry):
            acc = rows_ref[place_ref[t * top_count]].astype(jnp.float32)
            for k in range(1, top_count):
                acc = acc + rows_ref[place_ref[t * top_count + k]].astype(jnp.float32)
            out_ref[t] = acc.astype(out_ref.dtype)
            return carry

        lax.fori_loop(0, tok_rows, one_token, 0, unroll=4)

    return pl.pallas_call(
        kernel,
        out_shape=jax.ShapeDtypeStruct((tok_rows,) + rows.shape[1:], jnp.bfloat16),
        in_specs=[
            pl.BlockSpec(memory_space=pltpu.SMEM),
            pl.BlockSpec(memory_space=pltpu.VMEM),
        ],
        out_specs=pl.BlockSpec(memory_space=pltpu.VMEM),
    )(place, rows)


def gather_tiles(row_of, src3, block, scale=None):
    total = row_of.shape[0]

    def kernel(row_ref, *refs):
        if scale is None:
            src_ref, out_ref = refs
        else:
            scale_ref, src_ref, out_ref = refs
        base = pl.program_id(0) * block

        def one_slot(i, carry):
            if scale is None:
                out_ref[i] = src_ref[row_ref[base + i]]
            else:
                row = src_ref[row_ref[base + i]].astype(jnp.float32) * scale_ref[base + i]
                out_ref[i] = row.astype(out_ref.dtype)
            return carry

        lax.fori_loop(0, block, one_slot, 0, unroll=8)

    src_spec = pl.BlockSpec(src3.shape, lambda g, rows: (0, 0, 0))
    in_specs = [src_spec] if scale is None else [pl.BlockSpec(memory_space=pltpu.SMEM), src_spec]
    operands = (row_of, src3) if scale is None else (row_of, scale, src3)
    return pl.pallas_call(
        kernel,
        out_shape=jax.ShapeDtypeStruct((total,) + src3.shape[1:], src3.dtype),
        grid_spec=pltpu.PrefetchScalarGridSpec(
            num_scalar_prefetch=1,
            grid=(total // block,),
            in_specs=in_specs,
            out_specs=pl.BlockSpec((block,) + src3.shape[1:], lambda g, rows: (g, 0, 0)),
        ),
    )(*operands)


def body(tokens, cotangent, gates, experts, owner, swapped, w_gate, w_up, w_down):
    tok_rows, width = tokens.shape
    top_count = experts.shape[1]
    expert_total = owner.shape[0]
    count = lax.axis_size("ep")
    slots = tok_rows * top_count * 3 // (2 * expert_total)
    pairs = tok_rows * top_count
    sub = width // LANES
    pair_slots = jnp.arange(swapped.shape[0], dtype=jnp.int32)
    flag = jnp.sum(
        jnp.where((owner // 2)[:, None] == pair_slots[None, :], swapped[None, :], 0), axis=1
    )
    holder = owner + flag * (1 - 2 * (owner % 2))
    wg = w_gate[0]
    wu = w_up[0]
    wd = w_down[0]
    flat_e = experts.reshape(-1)
    chosen = flat_e[:, None] == jnp.arange(expert_total, dtype=jnp.int32)[None, :]
    target = jnp.sum(jnp.where(chosen, holder[None, :], 0), axis=1)
    pair_ids = jnp.arange(pairs, dtype=jnp.int32)
    earlier = (target[None, :] == target[:, None]) & (pair_ids[None, :] < pair_ids[:, None])
    rank = jnp.sum(earlier.astype(jnp.int32), axis=1)
    place = target * slots + rank
    slot_ids = jnp.arange(count * slots, dtype=jnp.int32)
    match = place[None, :] == slot_ids[:, None]
    source = jnp.min(jnp.where(match, pair_ids[None, :], pairs), axis=1)
    gate_slot = jnp.sum(jnp.where(match, gates.reshape(-1)[None, :], 0.0), axis=1)
    row_of = source // top_count
    row_clamped = jnp.minimum(row_of, tok_rows - 1)
    send_x = gather_tiles(
        row_clamped, tokens.reshape(tok_rows, sub, LANES), 256
    ).reshape(count, slots, sub, LANES)
    send_c = gather_tiles(
        row_clamped, cotangent.reshape(tok_rows, sub, LANES), 256, gate_slot
    ).reshape(count, slots, sub, LANES)
    recv_x = lax.all_to_all(send_x, "ep", split_axis=0, concat_axis=0, tiled=True)
    recv_c = lax.all_to_all(send_c, "ep", split_axis=0, concat_axis=0, tiled=True)
    flat = recv_x.reshape(-1, width)
    act_a, act_b = project_in(flat, wg, wu)
    out_rows = project_out(act_a, act_b, wd)
    back = lax.all_to_all(
        out_rows.reshape(count, slots, sub, LANES), "ep", split_axis=0, concat_axis=0, tiled=True
    )
    pair_grad = project_back(recv_c.reshape(-1, width), act_a, act_b, wg, wu, wd)
    grad_back = lax.all_to_all(
        pair_grad.reshape(count, slots, sub, LANES), "ep", split_axis=0, concat_axis=0, tiled=True
    )
    out_pairs = (
        back.reshape(-1, sub, LANES)[place]
        .reshape(tok_rows, top_count, sub, LANES)
        .astype(jnp.float32)
    )
    mixed = jnp.sum(gates[:, :, None, None] * out_pairs, axis=1).astype(jnp.bfloat16)
    cot_f = cotangent.reshape(tok_rows, 1, sub, LANES).astype(jnp.float32)
    gate_grad = jnp.sum(cot_f * out_pairs, axis=(2, 3))
    in_grad = combine_rows(place, grad_back.reshape(-1, sub, LANES), tok_rows, top_count)
    return (mixed.reshape(tok_rows, width), in_grad.reshape(tok_rows, width), gate_grad)


def solution(mesh):
    return jax.shard_map(
        body,
        mesh=mesh,
        in_specs=(
            P("ep", None),
            P("ep", None),
            P("ep", None),
            P("ep", None),
            P(),
            P(),
            P("ep", None, None),
            P("ep", None, None),
            P("ep", None, None),
        ),
        out_specs=(P("ep", None), P("ep", None), P("ep", None)),
        check_vma=False,
    )
```

```python
import jax
import jax.numpy as jnp
from jax import lax
from jax.sharding import PartitionSpec as P
from jax.experimental import pallas as pl
from jax.experimental.pallas import tpu as pltpu

LANES = 128


def project_in(flat, wg, wu):
    act_a = jnp.dot(flat, wg, preferred_element_type=jnp.float32)
    act_b = jnp.dot(flat, wu, preferred_element_type=jnp.float32)
    return (act_a, act_b)


def project_out(act_a, act_b, wd):
    sig = jax.nn.sigmoid(act_a)
    hidden = (act_a * sig * act_b).astype(jnp.bfloat16)
    return jnp.dot(hidden, wd, preferred_element_type=jnp.float32).astype(jnp.bfloat16)


def project_back(cots, act_a, act_b, wg, wu, wd):
    sig = jax.nn.sigmoid(act_a)
    back_hidden = lax.dot_general(
        cots, wd, (((1,), (1,)), ((), ())), preferred_element_type=jnp.float32
    )
    grad_a = (back_hidden * act_b * sig * (1.0 + act_a * (1.0 - sig))).astype(jnp.bfloat16)
    grad_b = (back_hidden * act_a * sig).astype(jnp.bfloat16)
    pair_grad = lax.dot_general(
        grad_a, wg, (((1,), (1,)), ((), ())), preferred_element_type=jnp.float32
    )
    pair_grad = pair_grad + lax.dot_general(
        grad_b, wu, (((1,), (1,)), ((), ())), preferred_element_type=jnp.float32
    )
    return pair_grad.astype(jnp.bfloat16)


def combine_rows(place, rows, tok_rows, top_count):
    def kernel(place_ref, rows_ref, out_ref):
        def one_token(t, carry):
            acc = rows_ref[place_ref[t * top_count]].astype(jnp.float32)
            for k in range(1, top_count):
                acc = acc + rows_ref[place_ref[t * top_count + k]].astype(jnp.float32)
            out_ref[t] = acc.astype(out_ref.dtype)
            return carry

        lax.fori_loop(0, tok_rows, one_token, 0, unroll=8)

    return pl.pallas_call(
        kernel,
        out_shape=jax.ShapeDtypeStruct((tok_rows,) + rows.shape[1:], jnp.bfloat16),
        in_specs=[
            pl.BlockSpec(memory_space=pltpu.SMEM),
            pl.BlockSpec(memory_space=pltpu.VMEM),
        ],
        out_specs=pl.BlockSpec(memory_space=pltpu.VMEM),
    )(place, rows)


def gather_tiles(row_of, src3, block, scale=None):
    total = row_of.shape[0]

    def kernel(row_ref, *refs):
        if scale is None:
            src_ref, out_ref = refs
        else:
            scale_ref, src_ref, out_ref = refs
        base = pl.program_id(0) * block

        def one_slot(i, carry):
            if scale is None:
                out_ref[i] = src_ref[row_ref[base + i]]
            else:
                row = src_ref[row_ref[base + i]].astype(jnp.float32) * scale_ref[base + i]
                out_ref[i] = row.astype(out_ref.dtype)
            return carry

        lax.fori_loop(0, block, one_slot, 0, unroll=16)

    src_spec = pl.BlockSpec(src3.shape, lambda g, rows: (0, 0, 0))
    in_specs = [src_spec] if scale is None else [pl.BlockSpec(memory_space=pltpu.SMEM), src_spec]
    operands = (row_of, src3) if scale is None else (row_of, scale, src3)
    return pl.pallas_call(
        kernel,
        out_shape=jax.ShapeDtypeStruct((total,) + src3.shape[1:], src3.dtype),
        grid_spec=pltpu.PrefetchScalarGridSpec(
            num_scalar_prefetch=1,
            grid=(total // block,),
            in_specs=in_specs,
            out_specs=pl.BlockSpec((block,) + src3.shape[1:], lambda g, rows: (g, 0, 0)),
        ),
    )(*operands)


def body(tokens, cotangent, gates, experts, owner, swapped, w_gate, w_up, w_down):
    tok_rows, width = tokens.shape
    top_count = experts.shape[1]
    expert_total = owner.shape[0]
    count = lax.axis_size("ep")
    slots = tok_rows * top_count * 3 // (2 * expert_total)
    pairs = tok_rows * top_count
    sub = width // LANES
    pair_slots = jnp.arange(swapped.shape[0], dtype=jnp.int32)
    flag = jnp.sum(
        jnp.where((owner // 2)[:, None] == pair_slots[None, :], swapped[None, :], 0), axis=1
    )
    holder = owner + flag * (1 - 2 * (owner % 2))
    wg = w_gate[0]
    wu = w_up[0]
    wd = w_down[0]
    flat_e = experts.reshape(-1)
    chosen = flat_e[:, None] == jnp.arange(expert_total, dtype=jnp.int32)[None, :]
    target = jnp.sum(jnp.where(chosen, holder[None, :], 0), axis=1)
    pair_ids = jnp.arange(pairs, dtype=jnp.int32)
    earlier = (target[None, :] == target[:, None]) & (pair_ids[None, :] < pair_ids[:, None])
    rank = jnp.sum(earlier.astype(jnp.int32), axis=1)
    place = target * slots + rank
    slot_ids = jnp.arange(count * slots, dtype=jnp.int32)
    match = place[None, :] == slot_ids[:, None]
    source = jnp.min(jnp.where(match, pair_ids[None, :], pairs), axis=1)
    gate_slot = jnp.sum(jnp.where(match, gates.reshape(-1)[None, :], 0.0), axis=1)
    row_of = source // top_count
    row_clamped = jnp.minimum(row_of, tok_rows - 1)
    send_x = gather_tiles(
        row_clamped, tokens.reshape(tok_rows, sub, LANES), 256
    ).reshape(count, slots, sub, LANES)
    send_c = gather_tiles(
        row_clamped, cotangent.reshape(tok_rows, sub, LANES), 256, gate_slot
    ).reshape(count, slots, sub, LANES)
    recv_x = lax.all_to_all(send_x, "ep", split_axis=0, concat_axis=0, tiled=True)
    recv_c = lax.all_to_all(send_c, "ep", split_axis=0, concat_axis=0, tiled=True)
    flat = recv_x.reshape(-1, width)
    act_a, act_b = project_in(flat, wg, wu)
    out_rows = project_out(act_a, act_b, wd)
    back = lax.all_to_all(
        out_rows.reshape(count, slots, sub, LANES), "ep", split_axis=0, concat_axis=0, tiled=True
    )
    pair_grad = project_back(recv_c.reshape(-1, width), act_a, act_b, wg, wu, wd)
    grad_back = lax.all_to_all(
        pair_grad.reshape(count, slots, sub, LANES), "ep", split_axis=0, concat_axis=0, tiled=True
    )
    out_pairs = (
        back.reshape(-1, sub, LANES)[place]
        .reshape(tok_rows, top_count, sub, LANES)
        .astype(jnp.float32)
    )
    mixed = jnp.sum(gates[:, :, None, None] * out_pairs, axis=1).astype(jnp.bfloat16)
    cot_f = cotangent.reshape(tok_rows, 1, sub, LANES).astype(jnp.float32)
    gate_grad = jnp.sum(cot_f * out_pairs, axis=(2, 3))
    in_grad = combine_rows(place, grad_back.reshape(-1, sub, LANES), tok_rows, top_count)
    return (mixed.reshape(tok_rows, width), in_grad.reshape(tok_rows, width), gate_grad)


def solution(mesh):
    return jax.shard_map(
        body,
        mesh=mesh,
        in_specs=(
            P("ep", None),
            P("ep", None),
            P("ep", None),
            P("ep", None),
            P(),
            P(),
            P("ep", None, None),
            P("ep", None, None),
            P("ep", None, None),
        ),
        out_specs=(P("ep", None), P("ep", None), P("ep", None)),
        check_vma=False,
    )
```

```python
import jax
import jax.numpy as jnp
from jax import lax
from jax.sharding import PartitionSpec as P
from jax.experimental import pallas as pl
from jax.experimental.pallas import tpu as pltpu

LANES = 128


def project_in(flat, wg, wu):
    act_a = jnp.dot(flat, wg, preferred_element_type=jnp.float32)
    act_b = jnp.dot(flat, wu, preferred_element_type=jnp.float32)
    return (act_a, act_b)


def project_out(act_a, act_b, wd):
    sig = jax.nn.sigmoid(act_a)
    hidden = (act_a * sig * act_b).astype(jnp.bfloat16)
    return jnp.dot(hidden, wd, preferred_element_type=jnp.float32).astype(jnp.bfloat16)


def project_back(cots, act_a, act_b, wg, wu, wd):
    sig = jax.nn.sigmoid(act_a)
    back_hidden = lax.dot_general(
        cots, wd, (((1,), (1,)), ((), ())), preferred_element_type=jnp.float32
    )
    grad_a = (back_hidden * act_b * sig * (1.0 + act_a * (1.0 - sig))).astype(jnp.bfloat16)
    grad_b = (back_hidden * act_a * sig).astype(jnp.bfloat16)
    pair_grad = lax.dot_general(
        grad_a, wg, (((1,), (1,)), ((), ())), preferred_element_type=jnp.float32
    )
    pair_grad = pair_grad + lax.dot_general(
        grad_b, wu, (((1,), (1,)), ((), ())), preferred_element_type=jnp.float32
    )
    return pair_grad.astype(jnp.bfloat16)


def combine_rows(place, rows, tok_rows, top_count):
    def kernel(place_ref, rows_ref, out_ref):
        def one_token(t, carry):
            acc = rows_ref[place_ref[t]].astype(jnp.float32)
            for k in range(1, top_count):
                acc = acc + rows_ref[place_ref[k * tok_rows + t]].astype(jnp.float32)
            out_ref[t] = acc.astype(out_ref.dtype)
            return carry

        lax.fori_loop(0, tok_rows, one_token, 0, unroll=8)

    return pl.pallas_call(
        kernel,
        out_shape=jax.ShapeDtypeStruct((tok_rows,) + rows.shape[1:], jnp.bfloat16),
        in_specs=[
            pl.BlockSpec(memory_space=pltpu.SMEM),
            pl.BlockSpec(memory_space=pltpu.VMEM),
        ],
        out_specs=pl.BlockSpec(memory_space=pltpu.VMEM),
    )(place, rows)


def gather_tiles(row_of, src3, block, scale=None):
    total = row_of.shape[0]

    def kernel(row_ref, *refs):
        if scale is None:
            src_ref, out_ref = refs
        else:
            scale_ref, src_ref, out_ref = refs
        base = pl.program_id(0) * block

        def one_slot(i, carry):
            if scale is None:
                out_ref[i] = src_ref[row_ref[base + i]]
            else:
                row = src_ref[row_ref[base + i]].astype(jnp.float32) * scale_ref[base + i]
                out_ref[i] = row.astype(out_ref.dtype)
            return carry

        lax.fori_loop(0, block, one_slot, 0, unroll=16)

    src_spec = pl.BlockSpec(src3.shape, lambda g, rows: (0, 0, 0))
    in_specs = [src_spec] if scale is None else [pl.BlockSpec(memory_space=pltpu.SMEM), src_spec]
    operands = (row_of, src3) if scale is None else (row_of, scale, src3)
    return pl.pallas_call(
        kernel,
        out_shape=jax.ShapeDtypeStruct((total,) + src3.shape[1:], src3.dtype),
        grid_spec=pltpu.PrefetchScalarGridSpec(
            num_scalar_prefetch=1,
            grid=(total // block,),
            in_specs=in_specs,
            out_specs=pl.BlockSpec((block,) + src3.shape[1:], lambda g, rows: (g, 0, 0)),
        ),
    )(*operands)


def body(tokens, cotangent, gates, experts, owner, swapped, w_gate, w_up, w_down):
    tok_rows, width = tokens.shape
    top_count = experts.shape[1]
    expert_total = owner.shape[0]
    count = lax.axis_size("ep")
    slots = tok_rows * top_count * 3 // (2 * expert_total)
    pairs = tok_rows * top_count
    sub = width // LANES
    pair_slots = jnp.arange(swapped.shape[0], dtype=jnp.int32)
    flag = jnp.sum(
        jnp.where((owner // 2)[:, None] == pair_slots[None, :], swapped[None, :], 0), axis=1
    )
    holder = owner + flag * (1 - 2 * (owner % 2))
    wg = w_gate[0]
    wu = w_up[0]
    wd = w_down[0]
    flat_e = experts.T.reshape(-1)
    chosen = flat_e[:, None] == jnp.arange(expert_total, dtype=jnp.int32)[None, :]
    target = jnp.sum(jnp.where(chosen, holder[None, :], 0), axis=1)
    pair_ids = jnp.arange(pairs, dtype=jnp.int32)
    earlier = (target[None, :] == target[:, None]) & (pair_ids[None, :] < pair_ids[:, None])
    rank = jnp.sum(earlier.astype(jnp.int32), axis=1)
    place = target * slots + rank
    slot_ids = jnp.arange(count * slots, dtype=jnp.int32)
    match = place[None, :] == slot_ids[:, None]
    source = jnp.min(jnp.where(match, pair_ids[None, :], pairs), axis=1)
    gate_slot = jnp.sum(jnp.where(match, gates.T.reshape(-1)[None, :], 0.0), axis=1)
    row_of = source % tok_rows
    row_clamped = jnp.minimum(row_of, tok_rows - 1)
    send_x = gather_tiles(
        row_clamped, tokens.reshape(tok_rows, sub, LANES), 256
    ).reshape(count, slots, sub, LANES)
    send_c = gather_tiles(
        row_clamped, cotangent.reshape(tok_rows, sub, LANES), 256, gate_slot
    ).reshape(count, slots, sub, LANES)
    recv_x = lax.all_to_all(send_x, "ep", split_axis=0, concat_axis=0, tiled=True)
    recv_c = lax.all_to_all(send_c, "ep", split_axis=0, concat_axis=0, tiled=True)
    flat = recv_x.reshape(-1, width)
    act_a, act_b = project_in(flat, wg, wu)
    out_rows = project_out(act_a, act_b, wd)
    back = lax.all_to_all(
        out_rows.reshape(count, slots, sub, LANES), "ep", split_axis=0, concat_axis=0, tiled=True
    )
    pair_grad = project_back(recv_c.reshape(-1, width), act_a, act_b, wg, wu, wd)
    grad_back = lax.all_to_all(
        pair_grad.reshape(count, slots, sub, LANES), "ep", split_axis=0, concat_axis=0, tiled=True
    )
    out_pairs = (
        back.reshape(-1, sub, LANES)[place]
        .reshape(top_count, tok_rows, sub, LANES)
        .astype(jnp.float32)
    )
    mixed = jnp.sum(gates.T[:, :, None, None] * out_pairs, axis=0).astype(jnp.bfloat16)
    cot_f = cotangent.reshape(1, tok_rows, sub, LANES).astype(jnp.float32)
    gate_grad = jnp.sum(cot_f * out_pairs, axis=(2, 3)).T
    in_grad = combine_rows(place, grad_back.reshape(-1, sub, LANES), tok_rows, top_count)
    return (mixed.reshape(tok_rows, width), in_grad.reshape(tok_rows, width), gate_grad)


def solution(mesh):
    return jax.shard_map(
        body,
        mesh=mesh,
        in_specs=(
            P("ep", None),
            P("ep", None),
            P("ep", None),
            P("ep", None),
            P(),
            P(),
            P("ep", None, None),
            P("ep", None, None),
            P("ep", None, None),
        ),
        out_specs=(P("ep", None), P("ep", None), P("ep", None)),
        check_vma=False,
    )
```

```python
import jax
import jax.numpy as jnp
from jax import lax
from jax.sharding import PartitionSpec as P
from jax.experimental import pallas as pl
from jax.experimental.pallas import tpu as pltpu

LANES = 128


def project_in(flat, wg, wu):
    act_a = jnp.dot(flat, wg, preferred_element_type=jnp.float32)
    act_b = jnp.dot(flat, wu, preferred_element_type=jnp.float32)
    return (act_a, act_b)


def project_out(act_a, act_b, wd):
    sig = jax.nn.sigmoid(act_a)
    hidden = (act_a * sig * act_b).astype(jnp.bfloat16)
    return jnp.dot(hidden, wd, preferred_element_type=jnp.float32).astype(jnp.bfloat16)


def project_back(cots, act_a, act_b, wg, wu, wd):
    sig = jax.nn.sigmoid(act_a)
    back_hidden = lax.dot_general(
        cots, wd, (((1,), (1,)), ((), ())), preferred_element_type=jnp.float32
    )
    grad_a = (back_hidden * act_b * sig * (1.0 + act_a * (1.0 - sig))).astype(jnp.bfloat16)
    grad_b = (back_hidden * act_a * sig).astype(jnp.bfloat16)
    pair_grad = lax.dot_general(
        grad_a, wg, (((1,), (1,)), ((), ())), preferred_element_type=jnp.float32
    )
    pair_grad = pair_grad + lax.dot_general(
        grad_b, wu, (((1,), (1,)), ((), ())), preferred_element_type=jnp.float32
    )
    return pair_grad.astype(jnp.bfloat16)


def combine_rows(place, rows, tok_rows, top_count):
    def kernel(place_ref, rows_ref, out_ref):
        def token_sum(t):
            acc = rows_ref[place_ref[t * top_count]].astype(jnp.float32)
            for k in range(1, top_count):
                acc = acc + rows_ref[place_ref[t * top_count + k]].astype(jnp.float32)
            return acc

        def one_group(g, carry):
            base = pl.multiple_of(g * 8, 8)
            accs = [token_sum(base + j) for j in range(8)]
            for a in range(accs[0].shape[0]):
                block = jnp.concatenate([acc[a : a + 1, :] for acc in accs], axis=0)
                out_ref[pl.ds(base, 8), pl.ds(a * LANES, LANES)] = block
            return carry

        lax.fori_loop(0, tok_rows // 8, one_group, 0)

    return pl.pallas_call(
        kernel,
        out_shape=jax.ShapeDtypeStruct((tok_rows, rows.shape[1] * rows.shape[2]), jnp.float32),
        in_specs=[
            pl.BlockSpec(memory_space=pltpu.SMEM),
            pl.BlockSpec(memory_space=pltpu.VMEM),
        ],
        out_specs=pl.BlockSpec(memory_space=pltpu.VMEM),
    )(place, rows)


def gather_tiles(row_of, src3, block, scale=None):
    total = row_of.shape[0]

    def kernel(row_ref, *refs):
        if scale is None:
            src_ref, out_ref = refs
        else:
            scale_ref, src_ref, out_ref = refs
        base = pl.program_id(0) * block

        def one_slot(i, carry):
            if scale is None:
                out_ref[i] = src_ref[row_ref[base + i]]
            else:
                row = src_ref[row_ref[base + i]].astype(jnp.float32) * scale_ref[base + i]
                out_ref[i] = row.astype(out_ref.dtype)
            return carry

        lax.fori_loop(0, block, one_slot, 0, unroll=16)

    src_spec = pl.BlockSpec(src3.shape, lambda g, rows: (0, 0, 0))
    in_specs = [src_spec] if scale is None else [pl.BlockSpec(memory_space=pltpu.SMEM), src_spec]
    operands = (row_of, src3) if scale is None else (row_of, scale, src3)
    return pl.pallas_call(
        kernel,
        out_shape=jax.ShapeDtypeStruct((total,) + src3.shape[1:], src3.dtype),
        grid_spec=pltpu.PrefetchScalarGridSpec(
            num_scalar_prefetch=1,
            grid=(total // block,),
            in_specs=in_specs,
            out_specs=pl.BlockSpec((block,) + src3.shape[1:], lambda g, rows: (g, 0, 0)),
        ),
    )(*operands)


def body(tokens, cotangent, gates, experts, owner, swapped, w_gate, w_up, w_down):
    tok_rows, width = tokens.shape
    top_count = experts.shape[1]
    expert_total = owner.shape[0]
    count = lax.axis_size("ep")
    slots = tok_rows * top_count * 3 // (2 * expert_total)
    pairs = tok_rows * top_count
    sub = width // LANES
    pair_slots = jnp.arange(swapped.shape[0], dtype=jnp.int32)
    flag = jnp.sum(
        jnp.where((owner // 2)[:, None] == pair_slots[None, :], swapped[None, :], 0), axis=1
    )
    holder = owner + flag * (1 - 2 * (owner % 2))
    wg = w_gate[0]
    wu = w_up[0]
    wd = w_down[0]
    flat_e = experts.reshape(-1)
    chosen = flat_e[:, None] == jnp.arange(expert_total, dtype=jnp.int32)[None, :]
    target = jnp.sum(jnp.where(chosen, holder[None, :], 0), axis=1)
    pair_ids = jnp.arange(pairs, dtype=jnp.int32)
    earlier = (target[None, :] == target[:, None]) & (pair_ids[None, :] < pair_ids[:, None])
    rank = jnp.sum(earlier.astype(jnp.int32), axis=1)
    place = target * slots + rank
    slot_ids = jnp.arange(count * slots, dtype=jnp.int32)
    match = place[None, :] == slot_ids[:, None]
    source = jnp.min(jnp.where(match, pair_ids[None, :], pairs), axis=1)
    gate_slot = jnp.sum(jnp.where(match, gates.reshape(-1)[None, :], 0.0), axis=1)
    row_of = source // top_count
    row_clamped = jnp.minimum(row_of, tok_rows - 1)
    send_x = gather_tiles(
        row_clamped, tokens.reshape(tok_rows, sub, LANES), 256
    ).reshape(count, slots, sub, LANES)
    send_c = gather_tiles(
        row_clamped, cotangent.reshape(tok_rows, sub, LANES), 256, gate_slot
    ).reshape(count, slots, sub, LANES)
    recv_x = lax.all_to_all(send_x, "ep", split_axis=0, concat_axis=0, tiled=True)
    recv_c = lax.all_to_all(send_c, "ep", split_axis=0, concat_axis=0, tiled=True)
    flat = recv_x.reshape(-1, width)
    act_a, act_b = project_in(flat, wg, wu)
    out_rows = project_out(act_a, act_b, wd)
    back = lax.all_to_all(
        out_rows.reshape(count, slots, sub, LANES), "ep", split_axis=0, concat_axis=0, tiled=True
    )
    pair_grad = project_back(recv_c.reshape(-1, width), act_a, act_b, wg, wu, wd)
    grad_back = lax.all_to_all(
        pair_grad.reshape(count, slots, sub, LANES), "ep", split_axis=0, concat_axis=0, tiled=True
    )
    out_pairs = (
        back.reshape(-1, sub, LANES)[place]
        .reshape(tok_rows, top_count, sub, LANES)
        .astype(jnp.float32)
    )
    mixed = jnp.sum(gates[:, :, None, None] * out_pairs, axis=1).astype(jnp.bfloat16)
    cot_f = cotangent.reshape(tok_rows, 1, sub, LANES).astype(jnp.float32)
    gate_grad = jnp.sum(cot_f * out_pairs, axis=(2, 3))
    in_grad = combine_rows(place, grad_back.reshape(-1, sub, LANES), tok_rows, top_count).astype(
        jnp.bfloat16
    )
    return (mixed.reshape(tok_rows, width), in_grad.reshape(tok_rows, width), gate_grad)


def solution(mesh):
    return jax.shard_map(
        body,
        mesh=mesh,
        in_specs=(
            P("ep", None),
            P("ep", None),
            P("ep", None),
            P("ep", None),
            P(),
            P(),
            P("ep", None, None),
            P("ep", None, None),
            P("ep", None, None),
        ),
        out_specs=(P("ep", None), P("ep", None), P("ep", None)),
        check_vma=False,
    )
```

```python
import jax
import jax.numpy as jnp
from jax import lax
from jax.sharding import PartitionSpec as P
from jax.experimental import pallas as pl
from jax.experimental.pallas import tpu as pltpu

LANES = 128


def project_in(flat, wg, wu):
    act_a = jnp.dot(flat, wg, preferred_element_type=jnp.float32)
    act_b = jnp.dot(flat, wu, preferred_element_type=jnp.float32)
    return (act_a, act_b)


def project_out(act_a, act_b, wd):
    sig = jax.nn.sigmoid(act_a)
    hidden = (act_a * sig * act_b).astype(jnp.bfloat16)
    return jnp.dot(hidden, wd, preferred_element_type=jnp.float32).astype(jnp.bfloat16)


def project_back(cots, act_a, act_b, wg, wu, wd):
    sig = jax.nn.sigmoid(act_a)
    back_hidden = lax.dot_general(
        cots, wd, (((1,), (1,)), ((), ())), preferred_element_type=jnp.float32
    )
    grad_a = (back_hidden * act_b * sig * (1.0 + act_a * (1.0 - sig))).astype(jnp.bfloat16)
    grad_b = (back_hidden * act_a * sig).astype(jnp.bfloat16)
    pair_grad = lax.dot_general(
        grad_a, wg, (((1,), (1,)), ((), ())), preferred_element_type=jnp.float32
    )
    pair_grad = pair_grad + lax.dot_general(
        grad_b, wu, (((1,), (1,)), ((), ())), preferred_element_type=jnp.float32
    )
    return pair_grad.astype(jnp.bfloat16)


def combine_rows(place, rows, tok_rows, top_count):
    def kernel(place_ref, rows_ref, out_ref):
        def token_sum(t):
            acc = rows_ref[place_ref[t * top_count]].astype(jnp.float32)
            for k in range(1, top_count):
                acc = acc + rows_ref[place_ref[t * top_count + k]].astype(jnp.float32)
            return acc

        def one_group(g, carry):
            base = pl.multiple_of(g * 16, 16)
            accs = [token_sum(base + j) for j in range(16)]
            for a in range(accs[0].shape[0]):
                block = jnp.concatenate([acc[a : a + 1, :] for acc in accs], axis=0)
                out_ref[pl.ds(base, 16), pl.ds(a * LANES, LANES)] = block.astype(out_ref.dtype)
            return carry

        lax.fori_loop(0, tok_rows // 16, one_group, 0)

    return pl.pallas_call(
        kernel,
        out_shape=jax.ShapeDtypeStruct((tok_rows, rows.shape[1] * rows.shape[2]), jnp.bfloat16),
        in_specs=[
            pl.BlockSpec(memory_space=pltpu.SMEM),
            pl.BlockSpec(memory_space=pltpu.VMEM),
        ],
        out_specs=pl.BlockSpec(memory_space=pltpu.VMEM),
    )(place, rows)


def gather_tiles(row_of, src3, block, scale=None):
    total = row_of.shape[0]

    def kernel(row_ref, *refs):
        if scale is None:
            src_ref, out_ref = refs
        else:
            scale_ref, src_ref, out_ref = refs
        base = pl.program_id(0) * block

        def one_slot(i, carry):
            if scale is None:
                out_ref[i] = src_ref[row_ref[base + i]]
            else:
                row = src_ref[row_ref[base + i]].astype(jnp.float32) * scale_ref[base + i]
                out_ref[i] = row.astype(out_ref.dtype)
            return carry

        lax.fori_loop(0, block, one_slot, 0, unroll=16)

    src_spec = pl.BlockSpec(src3.shape, lambda g, rows: (0, 0, 0))
    in_specs = [src_spec] if scale is None else [pl.BlockSpec(memory_space=pltpu.SMEM), src_spec]
    operands = (row_of, src3) if scale is None else (row_of, scale, src3)
    return pl.pallas_call(
        kernel,
        out_shape=jax.ShapeDtypeStruct((total,) + src3.shape[1:], src3.dtype),
        grid_spec=pltpu.PrefetchScalarGridSpec(
            num_scalar_prefetch=1,
            grid=(total // block,),
            in_specs=in_specs,
            out_specs=pl.BlockSpec((block,) + src3.shape[1:], lambda g, rows: (g, 0, 0)),
        ),
    )(*operands)


def body(tokens, cotangent, gates, experts, owner, swapped, w_gate, w_up, w_down):
    tok_rows, width = tokens.shape
    top_count = experts.shape[1]
    expert_total = owner.shape[0]
    count = lax.axis_size("ep")
    slots = tok_rows * top_count * 3 // (2 * expert_total)
    pairs = tok_rows * top_count
    sub = width // LANES
    pair_slots = jnp.arange(swapped.shape[0], dtype=jnp.int32)
    flag = jnp.sum(
        jnp.where((owner // 2)[:, None] == pair_slots[None, :], swapped[None, :], 0), axis=1
    )
    holder = owner + flag * (1 - 2 * (owner % 2))
    wg = w_gate[0]
    wu = w_up[0]
    wd = w_down[0]
    flat_e = experts.reshape(-1)
    chosen = flat_e[:, None] == jnp.arange(expert_total, dtype=jnp.int32)[None, :]
    target = jnp.sum(jnp.where(chosen, holder[None, :], 0), axis=1)
    pair_ids = jnp.arange(pairs, dtype=jnp.int32)
    earlier = (target[None, :] == target[:, None]) & (pair_ids[None, :] < pair_ids[:, None])
    rank = jnp.sum(earlier.astype(jnp.int32), axis=1)
    place = target * slots + rank
    slot_ids = jnp.arange(count * slots, dtype=jnp.int32)
    match = place[None, :] == slot_ids[:, None]
    source = jnp.min(jnp.where(match, pair_ids[None, :], pairs), axis=1)
    gate_slot = jnp.sum(jnp.where(match, gates.reshape(-1)[None, :], 0.0), axis=1)
    row_of = source // top_count
    row_clamped = jnp.minimum(row_of, tok_rows - 1)
    send_x = gather_tiles(
        row_clamped, tokens.reshape(tok_rows, sub, LANES), 256
    ).reshape(count, slots, sub, LANES)
    send_c = gather_tiles(
        row_clamped, cotangent.reshape(tok_rows, sub, LANES), 256, gate_slot
    ).reshape(count, slots, sub, LANES)
    recv_x = lax.all_to_all(send_x, "ep", split_axis=0, concat_axis=0, tiled=True)
    recv_c = lax.all_to_all(send_c, "ep", split_axis=0, concat_axis=0, tiled=True)
    flat = recv_x.reshape(-1, width)
    act_a, act_b = project_in(flat, wg, wu)
    out_rows = project_out(act_a, act_b, wd)
    back = lax.all_to_all(
        out_rows.reshape(count, slots, sub, LANES), "ep", split_axis=0, concat_axis=0, tiled=True
    )
    pair_grad = project_back(recv_c.reshape(-1, width), act_a, act_b, wg, wu, wd)
    grad_back = lax.all_to_all(
        pair_grad.reshape(count, slots, sub, LANES), "ep", split_axis=0, concat_axis=0, tiled=True
    )
    out_pairs = (
        back.reshape(-1, sub, LANES)[place]
        .reshape(tok_rows, top_count, sub, LANES)
        .astype(jnp.float32)
    )
    mixed = jnp.sum(gates[:, :, None, None] * out_pairs, axis=1).astype(jnp.bfloat16)
    cot_f = cotangent.reshape(tok_rows, 1, sub, LANES).astype(jnp.float32)
    gate_grad = jnp.sum(cot_f * out_pairs, axis=(2, 3))
    in_grad = combine_rows(place, grad_back.reshape(-1, sub, LANES), tok_rows, top_count)
    return (mixed.reshape(tok_rows, width), in_grad.reshape(tok_rows, width), gate_grad)


def solution(mesh):
    return jax.shard_map(
        body,
        mesh=mesh,
        in_specs=(
            P("ep", None),
            P("ep", None),
            P("ep", None),
            P("ep", None),
            P(),
            P(),
            P("ep", None, None),
            P("ep", None, None),
            P("ep", None, None),
        ),
        out_specs=(P("ep", None), P("ep", None), P("ep", None)),
        check_vma=False,
    )
```
